128 devices in a mesh: gx: 4 (over z), gy: 16 (over x, y_lo, core), gz: 2 (over y_hi).
Axes of the slice: x: 4, y: 4 (y_hi: 2, y_lo: 2; y = y_hi * 2 + y_lo), z: 4, core: 2. Of those that a mesh axis runs over, the one named last changes fastest.
Arguments:
- right_side: float32 [64, 1024, 512], P('gx', 'gy', 'gz'), may hold values from -4 to 4
- initial_guess: float32 [64, 1024, 512], P('gx', 'gy', 'gz'), may hold values from -3 to 3
- damping: float32 [64, 1024, 512], P('gx', 'gy', 'gz'), may hold values from 0.1 to 4
- group_map: int32 [16, 256, 128], P('gx', 'gy', 'gz'), may hold values from 0 to 1023
- block_inverse: float32 [1024, 1024], P('gy'), may hold values from -0.1875 to 0.1875
Outputs:
- fine_iterate: float32 [64, 1024, 512], P('gx', 'gy', 'gz')
- middle_correction: float32 [32, 512, 256], P('gx', 'gy', 'gz')
- coarse_correction: float32 [16, 256, 128], P('gx', 'gy', 'gz')
- aggregate_solution: float32 [1024], P('gy')
The draws below stay inside these ranges and needn't reach their ends.
All inputs are finite; a program needn't handle non-finite values.
Results may differ from the reference program's by a relative error of at most 0.0003.
Values sent between devices are 32-bit elements; how exact they have to be, the bound alone decides.
No kernel may reach another device: no remote copies, remote signals or barrier semaphores. Data moves between devices by JAX's collectives and lax.ppermute only.
A program may use at most 192 MiB of HBM per device.

```python
import math
import jax
import jax.numpy as jnp
from jax import lax

SWEEPS = 4
NAGG = 1024
NX = 64
NY = 1024
NZ = 512
GROUP_CELLS = 512


def draw_right_side(key, part):
    return jax.random.truncated_normal(key, -4.0, 4.0, (NX, NY, NZ), jnp.float32)


def with_ends(result, key, smallest, largest):
    shape = result.shape
    place = [jax.random.randint(jax.random.fold_in(key, axis), (), 0, shape[axis]) for axis in range(len(shape))]
    result = result.at[tuple(place)].set(smallest)
    longest = shape.index(max(shape))
    place[longest] = (place[longest] + 1) % shape[longest]
    return result.at[tuple(place)].set(largest)


def steps_of(key, dims, shards, smallest, top_value):
    def one(axis_at, shards_of):
        steps = jax.random.uniform(jax.random.fold_in(jax.random.fold_in(key, 6), axis_at), (shards_of,), jnp.float32, smallest / len(shards), top_value / len(shards))
        return jnp.repeat(jnp.exp(steps), dims[axis_at] // shards_of).reshape((-1,) + (1,) * (len(dims) - axis_at - 1))

    factor_of = one(*shards[0])
    for cut in shards[1:]:
        factor_of = factor_of * one(*cut)
    return factor_of


def bell_draw(key, extent, scale, reach, shards=(), kind=jnp.bfloat16):
    values = scale * jax.random.normal(key, extent, jnp.float32)
    if shards:
        values = values * steps_of(key, extent, shards, -0.22, 0.18)
    return jnp.clip(values, -reach, reach).astype(kind)


def setup_inputs(seed: int = 0) -> dict:
    streams_of = jax.random.split(jax.random.key(seed), 6)
    right_side = draw_right_side(jax.random.fold_in(streams_of[5], 71), 0)
    initial_guess = bell_draw(streams_of[1], (NX, NY, NZ), 0.5, 3.0, ((0, 4), (1, 16), (2, 2)), jnp.float32)
    damping = jnp.clip(jnp.exp(math.log(4.0) - 3.6888794 * jax.random.uniform(streams_of[2], (NX, NY, NZ), jnp.float32) ** steps_of(streams_of[2], (NX, NY, NZ), ((0, 4), (1, 16), (2, 2)), -0.2, 0.2)), 0.1, 4.0)
    group_map = with_ends(jax.random.randint(streams_of[3], (NX // 4, NY // 4, NZ // 4), 0, NAGG), jax.random.fold_in(streams_of[3], 1), 0, NAGG - 1).astype(jnp.int32)
    block_inverse = bell_draw(streams_of[4], (NAGG, NAGG), NAGG ** -0.5, 0.1875, ((0, 16),), jnp.float32)
    return {"right_side": right_side, "initial_guess": initial_guess, "damping": damping, "group_map": group_map, "block_inverse": block_inverse}


OMEGA = 0.8

def neighbours(padded):
    total = padded[2:, 1:-1, 1:-1] + padded[:-2, 1:-1, 1:-1]
    total = total + padded[1:-1, 2:, 1:-1] + padded[1:-1, :-2, 1:-1]
    return total + padded[1:-1, 1:-1, 2:] + padded[1:-1, 1:-1, :-2]

def relax(padded, source, diagonal):
    centre = padded[1:-1, 1:-1, 1:-1]
    return centre + OMEGA * (source - (diagonal * centre - neighbours(padded))) / diagonal

def defect(padded, source, diagonal):
    centre = padded[1:-1, 1:-1, 1:-1]
    return source - (diagonal * centre - neighbours(padded))

def shrink(field):
    extent_a, extent_b, extent_c = field.shape
    blocks = field.reshape(extent_a // 2, 2, extent_b // 2, 2, extent_c // 2, 2)
    return blocks.sum(axis=(1, 3, 5)) * 0.125

def smooth(start, source, diagonal):
    current = start
    for sweep_count in range(SWEEPS):
        current = relax(jnp.pad(current, 1), source, diagonal)
    return current

def reference(right_side, initial_guess, damping, group_map, block_inverse):
    fine_diag = 6.0 + damping
    fine_iterate = smooth(initial_guess, right_side, fine_diag)
    fine_defect = defect(jnp.pad(fine_iterate, 1), right_side, fine_diag)
    middle_damp = 4.0 * shrink(damping)
    middle_source = 4.0 * shrink(fine_defect)
    middle_diag = 6.0 + middle_damp
    middle = smooth(jnp.zeros_like(middle_source), middle_source, middle_diag)
    middle_defect = defect(jnp.pad(middle, 1), middle_source, middle_diag)
    coarse_damp = 4.0 * shrink(middle_damp)
    coarse_source = 4.0 * shrink(middle_defect)
    coarse_diag = 6.0 + coarse_damp
    coarse = smooth(jnp.zeros_like(coarse_source), coarse_source, coarse_diag)
    coarse_defect = defect(jnp.pad(coarse, 1), coarse_source, coarse_diag)
    summed = jax.ops.segment_sum(coarse_defect.reshape(-1), group_map.reshape(-1), num_segments=NAGG)
    aggregate_source = summed / math.sqrt(GROUP_CELLS)
    solution = jnp.dot(block_inverse, aggregate_source, precision=lax.Precision.HIGHEST)
    return (fine_iterate, middle, coarse, solution)
```

```python
import math

import jax
import jax.numpy as jnp
from jax import lax
from jax.sharding import PartitionSpec as P

SWEEPS = 4
NAGG = 1024


OMEGA = 0.8


def with_halo(cells, sides, width):
    for axis, dim in sides:
        count = lax.axis_size(axis)
        ends = count - 1
        head = lax.slice_in_dim(cells, 0, width, axis=dim)
        tail = lax.slice_in_dim(cells, cells.shape[dim] - width, cells.shape[dim], axis=dim)
        cells = jnp.concatenate(
            [
                lax.ppermute(tail, axis, [(i, (i + 1) % count) for i in range(ends)]),
                cells,
                lax.ppermute(head, axis, [((i + 1) % count, i) for i in range(ends)]),
            ],
            axis=dim,
        )
    return cells


def neighbours(padded):
    total = padded[2:, 1:-1, 1:-1] + padded[:-2, 1:-1, 1:-1]
    total = total + padded[1:-1, 2:, 1:-1] + padded[1:-1, :-2, 1:-1]
    return total + padded[1:-1, 1:-1, 2:] + padded[1:-1, 1:-1, :-2]


def relax(padded, source, diagonal):
    centre = padded[1:-1, 1:-1, 1:-1]
    return centre + OMEGA * (source - (diagonal * centre - neighbours(padded))) / diagonal


def defect(padded, source, diagonal):
    centre = padded[1:-1, 1:-1, 1:-1]
    return source - (diagonal * centre - neighbours(padded))


def pair_matrix(rows, cols, along):
    row = lax.broadcasted_iota(jnp.int32, (rows, cols), 0)
    col = lax.broadcasted_iota(jnp.int32, (rows, cols), 1)
    if along == 0:
        return (col // 2 == row).astype(jnp.float32)
    return (row // 2 == col).astype(jnp.float32)


def shrink(field):
    extent_a, extent_b, extent_c = field.shape
    halves = field.reshape(extent_a // 2, 2, extent_b, extent_c)
    flat = (halves[:, 0] + halves[:, 1]).reshape(extent_a // 2 * extent_b, extent_c)
    rows = extent_a // 2 * extent_b
    flat = jnp.dot(pair_matrix(rows // 2, rows, 0), flat, precision=lax.Precision.HIGHEST)
    flat = jnp.dot(flat, pair_matrix(extent_c, extent_c // 2, 1), precision=lax.Precision.HIGHEST)
    return flat.reshape(extent_a // 2, extent_b // 2, extent_c // 2) * 0.125


def fine_rim(field):
    return with_halo(field, (("gx", 0), ("gy", 1), ("gz", 2)), 1)


def middle_rim(field):
    return with_halo(field, (("gx", 0), ("gy", 1), ("gz", 2)), 1)


def coarse_rim(field):
    return with_halo(field, (("gx", 0), ("gy", 1), ("gz", 2)), 1)


def shards(right_side, initial_guess, damping, group_map, block_inverse):
    fine_diag = 6.0 + damping
    iterate = initial_guess
    for sweep_count in range(SWEEPS):
        iterate = relax(fine_rim(iterate), right_side, fine_diag)
    fine_defect = defect(fine_rim(iterate), right_side, fine_diag)
    middle_damp = 4.0 * shrink(damping)
    middle_source = 4.0 * shrink(fine_defect)
    middle_diag = 6.0 + middle_damp
    middle = OMEGA * middle_source / middle_diag
    for sweep_count in range(SWEEPS - 1):
        middle = relax(middle_rim(middle), middle_source, middle_diag)
    middle_defect = defect(middle_rim(middle), middle_source, middle_diag)
    coarse_damp = 4.0 * shrink(middle_damp)
    coarse_source = 4.0 * shrink(middle_defect)
    coarse_diag = 6.0 + coarse_damp
    coarse = OMEGA * coarse_source / coarse_diag
    for sweep_count in range(SWEEPS - 1):
        coarse = relax(coarse_rim(coarse), coarse_source, coarse_diag)
    coarse_defect = defect(coarse_rim(coarse), coarse_source, coarse_diag)
    cells = coarse_defect.size
    one_hot = (
        group_map.reshape(cells, 1) == lax.broadcasted_iota(jnp.int32, (cells, NAGG), 1)
    ).astype(jnp.float32)
    partial_sums = jnp.dot(
        coarse_defect.reshape(1, cells), one_hot, precision=lax.Precision.HIGHEST
    ).reshape(NAGG)
    summed = lax.psum(partial_sums, ("gx", "gy", "gz"))
    group_cells = (
        coarse_source.size * lax.axis_size("gx") * lax.axis_size("gy") * lax.axis_size("gz") // NAGG
    )
    aggregate_source = summed / math.sqrt(group_cells)
    solution = jnp.dot(block_inverse, aggregate_source, precision=lax.Precision.HIGHEST)
    return (iterate, middle, coarse, solution)


def solution(mesh):
    return jax.shard_map(
        shards,
        mesh=mesh,
        in_specs=(
            P("gx", "gy", "gz"),
            P("gx", "gy", "gz"),
            P("gx", "gy", "gz"),
            P("gx", "gy", "gz"),
            P("gy", None),
        ),
        out_specs=(P("gx", "gy", "gz"), P("gx", "gy", "gz"), P("gx", "gy", "gz"), P("gy")),
        check_vma=False,
    )
```

```python
import math

import jax
import jax.numpy as jnp
from jax import lax
from jax.sharding import PartitionSpec as P

SWEEPS = 4
NAGG = 1024


OMEGA = 0.8


def with_halo(cells, sides, width):
    for axis, dim in sides:
        count = lax.axis_size(axis)
        ends = count - 1
        head = lax.slice_in_dim(cells, 0, width, axis=dim)
        tail = lax.slice_in_dim(cells, cells.shape[dim] - width, cells.shape[dim], axis=dim)
        cells = jnp.concatenate(
            [
                lax.ppermute(tail, axis, [(i, (i + 1) % count) for i in range(ends)]),
                cells,
                lax.ppermute(head, axis, [((i + 1) % count, i) for i in range(ends)]),
            ],
            axis=dim,
        )
    return cells


def neighbours(padded):
    total = padded[2:, 1:-1, 1:-1] + padded[:-2, 1:-1, 1:-1]
    total = total + padded[1:-1, 2:, 1:-1] + padded[1:-1, :-2, 1:-1]
    return total + padded[1:-1, 1:-1, 2:] + padded[1:-1, 1:-1, :-2]


def relax(padded, source, diagonal):
    centre = padded[1:-1, 1:-1, 1:-1]
    return centre + OMEGA * (source - (diagonal * centre - neighbours(padded))) / diagonal


def defect(padded, source, diagonal):
    centre = padded[1:-1, 1:-1, 1:-1]
    return source - (diagonal * centre - neighbours(padded))


def pair_matrix(rows, cols, along):
    row = lax.broadcasted_iota(jnp.int32, (rows, cols), 0)
    col = lax.broadcasted_iota(jnp.int32, (rows, cols), 1)
    if along == 0:
        return (col // 2 == row).astype(jnp.float32)
    return (row // 2 == col).astype(jnp.float32)


def shrink(field):
    extent_a, extent_b, extent_c = field.shape
    halves = field.reshape(extent_a // 2, 2, extent_b, extent_c)
    flat = (halves[:, 0] + halves[:, 1]).reshape(extent_a // 2 * extent_b, extent_c)
    rows = extent_a // 2 * extent_b
    flat = jnp.dot(pair_matrix(rows // 2, rows, 0), flat, precision=lax.Precision.HIGHEST)
    flat = jnp.dot(flat, pair_matrix(extent_c, extent_c // 2, 1), precision=lax.Precision.HIGHEST)
    return flat.reshape(extent_a // 2, extent_b // 2, extent_c // 2) * 0.125


def exchange(stack, width):
    for axis, dim in (("gz", 3), ("gy", 2), ("gx", 1)):
        count = lax.axis_size(axis)
        head = lax.slice_in_dim(stack, 0, width, axis=dim)
        tail = lax.slice_in_dim(stack, stack.shape[dim] - width, stack.shape[dim], axis=dim)
        stack = jnp.concatenate(
            [
                lax.ppermute(tail, axis, [(i, i + 1) for i in range(count - 1)]),
                stack,
                lax.ppermute(head, axis, [(i + 1, i) for i in range(count - 1)]),
            ],
            axis=dim,
        )
    return stack


def inside(shape, width):
    masks = []
    for axis, extent in zip(("gx", "gy", "gz"), shape):
        place = lax.axis_index(axis) * extent - width
        place = place + lax.broadcasted_iota(jnp.int32, (extent + 2 * width,), 0)
        masks.append((place >= 0) & (place < extent * lax.axis_size(axis)))
    return masks[0][:, None, None] & masks[1][None, :, None] & masks[2][None, None, :]


def crop(field, k):
    if k == 0:
        return field
    return field[k:-k, k:-k, k:-k]


def smooth_wide(start, source, diagonal, mask, steps):
    current = start
    for step in range(1, steps + 1):
        current = relax(current, crop(source, step), crop(diagonal, step))
        current = jnp.where(crop(mask, step), current, 0.0)
    return current


def coarser_level(source, damp):
    width = SWEEPS
    wide = exchange(jnp.stack([source, damp]), width)
    wide_source = wide[0]
    wide_diag = 6.0 + wide[1]
    mask = inside(source.shape, width)
    start = jnp.where(mask, OMEGA * wide_source / wide_diag, 0.0)
    current = smooth_wide(start, wide_source, wide_diag, mask, SWEEPS - 1)
    return crop(current, 1), defect(current, source, 6.0 + damp)


def shards(right_side, initial_guess, damping, group_map, block_inverse):
    width = SWEEPS + 1
    wide = exchange(jnp.stack([initial_guess, right_side, damping]), width)
    wide_source = wide[1]
    wide_diag = 6.0 + wide[2]
    mask = inside(right_side.shape, width)
    current = smooth_wide(wide[0], wide_source, wide_diag, mask, SWEEPS)
    iterate = crop(current, 1)
    fine_defect = defect(current, right_side, 6.0 + damping)
    middle_damp = 4.0 * shrink(damping)
    middle_source = 4.0 * shrink(fine_defect)
    middle, middle_defect = coarser_level(middle_source, middle_damp)
    coarse_damp = 4.0 * shrink(middle_damp)
    coarse_source = 4.0 * shrink(middle_defect)
    coarse, coarse_defect = coarser_level(coarse_source, coarse_damp)
    cells = coarse_defect.size
    one_hot = (
        group_map.reshape(cells, 1) == lax.broadcasted_iota(jnp.int32, (cells, NAGG), 1)
    ).astype(jnp.float32)
    partial_sums = jnp.dot(
        coarse_defect.reshape(1, cells), one_hot, precision=lax.Precision.HIGHEST
    ).reshape(NAGG)
    summed = lax.psum(partial_sums, ("gx", "gy", "gz"))
    group_cells = (
        coarse_source.size * lax.axis_size("gx") * lax.axis_size("gy") * lax.axis_size("gz") // NAGG
    )
    aggregate_source = summed / math.sqrt(group_cells)
    solution = jnp.dot(block_inverse, aggregate_source, precision=lax.Precision.HIGHEST)
    return (iterate, middle, coarse, solution)


def solution(mesh):
    return jax.shard_map(
        shards,
        mesh=mesh,
        in_specs=(
            P("gx", "gy", "gz"),
            P("gx", "gy", "gz"),
            P("gx", "gy", "gz"),
            P("gx", "gy", "gz"),
            P("gy", None),
        ),
        out_specs=(P("gx", "gy", "gz"), P("gx", "gy", "gz"), P("gx", "gy", "gz"), P("gy")),
        check_vma=False,
    )
```

```python
import math

import jax
import jax.numpy as jnp
from jax import lax
from jax.sharding import PartitionSpec as P

SWEEPS = 4
NAGG = 1024


OMEGA = 0.8


def with_halo(cells, sides, width):
    for axis, dim in sides:
        count = lax.axis_size(axis)
        ends = count - 1
        head = lax.slice_in_dim(cells, 0, width, axis=dim)
        tail = lax.slice_in_dim(cells, cells.shape[dim] - width, cells.shape[dim], axis=dim)
        cells = jnp.concatenate(
            [
                lax.ppermute(tail, axis, [(i, (i + 1) % count) for i in range(ends)]),
                cells,
                lax.ppermute(head, axis, [((i + 1) % count, i) for i in range(ends)]),
            ],
            axis=dim,
        )
    return cells


def neighbours(padded):
    total = padded[2:, 1:-1, 1:-1] + padded[:-2, 1:-1, 1:-1]
    total = total + padded[1:-1, 2:, 1:-1] + padded[1:-1, :-2, 1:-1]
    return total + padded[1:-1, 1:-1, 2:] + padded[1:-1, 1:-1, :-2]


def relax(padded, source, diagonal):
    centre = padded[1:-1, 1:-1, 1:-1]
    return centre + OMEGA * (source - (diagonal * centre - neighbours(padded))) / diagonal


def defect(padded, source, diagonal):
    centre = padded[1:-1, 1:-1, 1:-1]
    return source - (diagonal * centre - neighbours(padded))


def pair_matrix(rows, cols, along):
    row = lax.broadcasted_iota(jnp.int32, (rows, cols), 0)
    col = lax.broadcasted_iota(jnp.int32, (rows, cols), 1)
    if along == 0:
        return (col // 2 == row).astype(jnp.float32)
    return (row // 2 == col).astype(jnp.float32)


def shrink(field):
    extent_a, extent_b, extent_c = field.shape
    halves = field.reshape(extent_a // 2, 2, extent_b, extent_c)
    flat = (halves[:, 0] + halves[:, 1]).reshape(extent_a // 2 * extent_b, extent_c)
    rows = extent_a // 2 * extent_b
    flat = jnp.dot(pair_matrix(rows // 2, rows, 0), flat, precision=lax.Precision.HIGHEST)
    flat = jnp.dot(flat, pair_matrix(extent_c, extent_c // 2, 1), precision=lax.Precision.HIGHEST)
    return flat.reshape(extent_a // 2, extent_b // 2, extent_c // 2) * 0.125


def exchange(stack, width):
    for axis, dim in (("gz", 3), ("gy", 2), ("gx", 1)):
        count = lax.axis_size(axis)
        head = lax.slice_in_dim(stack, 0, width, axis=dim)
        tail = lax.slice_in_dim(stack, stack.shape[dim] - width, stack.shape[dim], axis=dim)
        stack = jnp.concatenate(
            [
                lax.ppermute(tail, axis, [(i, i + 1) for i in range(count - 1)]),
                stack,
                lax.ppermute(head, axis, [(i + 1, i) for i in range(count - 1)]),
            ],
            axis=dim,
        )
    return stack


def inside(shape, width):
    masks = []
    for axis, extent in zip(("gx", "gy", "gz"), shape):
        place = lax.axis_index(axis) * extent - width
        place = place + lax.broadcasted_iota(jnp.int32, (extent + 2 * width,), 0)
        masks.append((place >= 0) & (place < extent * lax.axis_size(axis)))
    return masks[0][:, None, None] & masks[1][None, :, None] & masks[2][None, None, :]


def crop(field, k):
    if k == 0:
        return field
    return field[k:-k, k:-k, k:-k]


def smooth_wide(start, source, diagonal, mask, steps):
    current = start
    for step in range(1, steps + 1):
        current = relax(current, crop(source, step), crop(diagonal, step))
        current = jnp.where(crop(mask, step), current, 0.0)
    return current


def coarser_level(source, damp):
    width = SWEEPS
    wide = exchange(jnp.stack([source, damp]), width)
    wide_source = wide[0]
    wide_diag = 6.0 + wide[1]
    mask = inside(source.shape, width)
    start = jnp.where(mask, OMEGA * wide_source / wide_diag, 0.0)
    current = smooth_wide(start, wide_source, wide_diag, mask, SWEEPS - 1)
    return crop(current, 1), defect(current, source, 6.0 + damp)


def shards(right_side, initial_guess, damping, group_map, block_inverse):
    width = SWEEPS + 1
    wide = exchange(jnp.stack([initial_guess, right_side, damping]), width)
    wide_source = wide[1]
    wide_diag = 6.0 + wide[2]
    mask = inside(right_side.shape, width)
    current = smooth_wide(wide[0], wide_source, wide_diag, mask, SWEEPS)
    iterate = crop(current, 1)
    fine_defect = defect(current, right_side, 6.0 + damping)
    middle_damp = 4.0 * shrink(damping)
    middle_source = 4.0 * shrink(fine_defect)
    middle, middle_defect = coarser_level(middle_source, middle_damp)
    coarse_damp = 4.0 * shrink(middle_damp)
    coarse_source = 4.0 * shrink(middle_defect)
    coarse, coarse_defect = coarser_level(coarse_source, coarse_damp)
    cells = coarse_defect.size
    one_hot = (
        group_map.reshape(cells, 1) == lax.broadcasted_iota(jnp.int32, (cells, NAGG), 1)
    ).astype(jnp.float32)
    partial_sums = jnp.dot(
        coarse_defect.reshape(1, cells), one_hot, precision=lax.Precision.HIGHEST
    ).reshape(NAGG)
    summed = lax.psum(partial_sums, "gz")
    summed = lax.psum(summed, "gx")
    summed = lax.psum(summed, "gy")
    group_cells = (
        coarse_source.size * lax.axis_size("gx") * lax.axis_size("gy") * lax.axis_size("gz") // NAGG
    )
    aggregate_source = summed / math.sqrt(group_cells)
    solution = jnp.dot(block_inverse, aggregate_source, precision=lax.Precision.HIGHEST)
    return (iterate, middle, coarse, solution)


def solution(mesh):
    return jax.shard_map(
        shards,
        mesh=mesh,
        in_specs=(
            P("gx", "gy", "gz"),
            P("gx", "gy", "gz"),
            P("gx", "gy", "gz"),
            P("gx", "gy", "gz"),
            P("gy", None),
        ),
        out_specs=(P("gx", "gy", "gz"), P("gx", "gy", "gz"), P("gx", "gy", "gz"), P("gy")),
        check_vma=False,
    )
```

```python
import math

import jax
import jax.numpy as jnp
from jax import lax
from jax.sharding import PartitionSpec as P

SWEEPS = 4
NAGG = 1024


OMEGA = 0.8


def with_halo(cells, sides, width):
    for axis, dim in sides:
        count = lax.axis_size(axis)
        ends = count - 1
        head = lax.slice_in_dim(cells, 0, width, axis=dim)
        tail = lax.slice_in_dim(cells, cells.shape[dim] - width, cells.shape[dim], axis=dim)
        cells = jnp.concatenate(
            [
                lax.ppermute(tail, axis, [(i, (i + 1) % count) for i in range(ends)]),
                cells,
                lax.ppermute(head, axis, [((i + 1) % count, i) for i in range(ends)]),
            ],
            axis=dim,
        )
    return cells


def neighbours(padded):
    total = padded[2:, 1:-1, 1:-1] + padded[:-2, 1:-1, 1:-1]
    total = total + padded[1:-1, 2:, 1:-1] + padded[1:-1, :-2, 1:-1]
    return total + padded[1:-1, 1:-1, 2:] + padded[1:-1, 1:-1, :-2]


def relax(padded, source, diagonal):
    centre = padded[1:-1, 1:-1, 1:-1]
    return centre + OMEGA * (source - (diagonal * centre - neighbours(padded))) / diagonal


def defect(padded, source, diagonal):
    centre = padded[1:-1, 1:-1, 1:-1]
    return source - (diagonal * centre - neighbours(padded))


def pair_matrix(rows, cols, along):
    row = lax.broadcasted_iota(jnp.int32, (rows, cols), 0)
    col = lax.broadcasted_iota(jnp.int32, (rows, cols), 1)
    if along == 0:
        return (col // 2 == row).astype(jnp.float32)
    return (row // 2 == col).astype(jnp.float32)


def shrink(field):
    extent_a, extent_b, extent_c = field.shape
    halves = field.reshape(extent_a // 2, 2, extent_b, extent_c)
    flat = (halves[:, 0] + halves[:, 1]).reshape(extent_a // 2 * extent_b, extent_c)
    rows = extent_a // 2 * extent_b
    flat = jnp.dot(pair_matrix(rows // 2, rows, 0), flat, precision=lax.Precision.HIGHEST)
    flat = jnp.dot(flat, pair_matrix(extent_c, extent_c // 2, 1), precision=lax.Precision.HIGHEST)
    return flat.reshape(extent_a // 2, extent_b // 2, extent_c // 2) * 0.125


def exchange(stack, width):
    for axis, dim in (("gz", 3), ("gy", 2), ("gx", 1)):
        count = lax.axis_size(axis)
        head = lax.slice_in_dim(stack, 0, width, axis=dim)
        tail = lax.slice_in_dim(stack, stack.shape[dim] - width, stack.shape[dim], axis=dim)
        stack = jnp.concatenate(
            [
                lax.ppermute(tail, axis, [(i, i + 1) for i in range(count - 1)]),
                stack,
                lax.ppermute(head, axis, [(i + 1, i) for i in range(count - 1)]),
            ],
            axis=dim,
        )
    return stack


def inside(shape, width):
    masks = []
    for axis, extent in zip(("gx", "gy", "gz"), shape):
        place = lax.axis_index(axis) * extent - width
        place = place + lax.broadcasted_iota(jnp.int32, (extent + 2 * width,), 0)
        masks.append((place >= 0) & (place < extent * lax.axis_size(axis)))
    return masks[0][:, None, None] & masks[1][None, :, None] & masks[2][None, None, :]


def crop(field, k):
    if k == 0:
        return field
    return field[k:-k, k:-k, k:-k]


def smooth_wide(start, source, diagonal, mask, steps):
    current = start
    for step in range(1, steps + 1):
        current = relax(current, crop(source, step), crop(diagonal, step))
        current = jnp.where(crop(mask, step), current, 0.0)
    return current


def coarser_level(source, damp):
    width = SWEEPS
    wide = exchange(jnp.stack([source, damp]), width)
    wide_source = wide[0]
    wide_diag = 6.0 + wide[1]
    mask = inside(source.shape, width)
    start = jnp.where(mask, OMEGA * wide_source / wide_diag, 0.0)
    current = smooth_wide(start, wide_source, wide_diag, mask, SWEEPS - 1)
    return crop(current, 1), defect(current, source, 6.0 + damp)


def shards(right_side, initial_guess, damping, group_map, block_inverse):
    width = SWEEPS + 1
    wide = exchange(jnp.stack([initial_guess, right_side, damping]), width)
    wide_source = wide[1]
    wide_diag = 6.0 + wide[2]
    mask = inside(right_side.shape, width)
    current = smooth_wide(wide[0], wide_source, wide_diag, mask, SWEEPS)
    iterate = crop(current, 1)
    fine_defect = defect(current, right_side, 6.0 + damping)
    middle_damp = 4.0 * shrink(damping)
    middle_source = 4.0 * shrink(fine_defect)
    middle, middle_defect = coarser_level(middle_source, middle_damp)
    coarse_damp = 4.0 * shrink(middle_damp)
    coarse_source = 4.0 * shrink(middle_defect)
    coarse, coarse_defect = coarser_level(coarse_source, coarse_damp)
    cells = coarse_defect.size
    one_hot = (
        group_map.reshape(cells, 1) == lax.broadcasted_iota(jnp.int32, (cells, NAGG), 1)
    ).astype(jnp.float32)
    partial_sums = jnp.dot(
        coarse_defect.reshape(1, cells), one_hot, precision=lax.Precision.HIGHEST
    ).reshape(NAGG)
    summed = lax.psum(partial_sums, "gz")
    summed = lax.psum(summed, "gx")
    for stride, span in ((1, 2), (2, 2), (4, 4)):
        groups = [
            [base + stride * k for k in range(span)]
            for base in range(lax.axis_size("gy"))
            if base % (stride * span) < stride
        ]
        summed = lax.psum(summed, "gy", axis_index_groups=groups)
    group_cells = (
        coarse_source.size * lax.axis_size("gx") * lax.axis_size("gy") * lax.axis_size("gz") // NAGG
    )
    aggregate_source = summed / math.sqrt(group_cells)
    solution = jnp.dot(block_inverse, aggregate_source, precision=lax.Precision.HIGHEST)
    return (iterate, middle, coarse, solution)


def solution(mesh):
    return jax.shard_map(
        shards,
        mesh=mesh,
        in_specs=(
            P("gx", "gy", "gz"),
            P("gx", "gy", "gz"),
            P("gx", "gy", "gz"),
            P("gx", "gy", "gz"),
            P("gy", None),
        ),
        out_specs=(P("gx", "gy", "gz"), P("gx", "gy", "gz"), P("gx", "gy", "gz"), P("gy")),
        check_vma=False,
    )
```

```python
import math

import jax
import jax.numpy as jnp
from jax import lax
from jax.sharding import PartitionSpec as P

SWEEPS = 4
NAGG = 1024


OMEGA = 0.8


def with_halo(cells, sides, width):
    for axis, dim in sides:
        count = lax.axis_size(axis)
        ends = count - 1
        head = lax.slice_in_dim(cells, 0, width, axis=dim)
        tail = lax.slice_in_dim(cells, cells.shape[dim] - width, cells.shape[dim], axis=dim)
        cells = jnp.concatenate(
            [
                lax.ppermute(tail, axis, [(i, (i + 1) % count) for i in range(ends)]),
                cells,
                lax.ppermute(head, axis, [((i + 1) % count, i) for i in range(ends)]),
            ],
            axis=dim,
        )
    return cells


def neighbours(padded):
    total = padded[2:, 1:-1, 1:-1] + padded[:-2, 1:-1, 1:-1]
    total = total + padded[1:-1, 2:, 1:-1] + padded[1:-1, :-2, 1:-1]
    return total + padded[1:-1, 1:-1, 2:] + padded[1:-1, 1:-1, :-2]


def relax(padded, source, diagonal):
    centre = padded[1:-1, 1:-1, 1:-1]
    return centre + OMEGA * (source - (diagonal * centre - neighbours(padded))) / diagonal


def defect(padded, source, diagonal):
    centre = padded[1:-1, 1:-1, 1:-1]
    return source - (diagonal * centre - neighbours(padded))


def pair_matrix(rows, cols, along):
    row = lax.broadcasted_iota(jnp.int32, (rows, cols), 0)
    col = lax.broadcasted_iota(jnp.int32, (rows, cols), 1)
    if along == 0:
        return (col // 2 == row).astype(jnp.float32)
    return (row // 2 == col).astype(jnp.float32)


def shrink(field):
    extent_a, extent_b, extent_c = field.shape
    halves = field.reshape(extent_a // 2, 2, extent_b, extent_c)
    flat = (halves[:, 0] + halves[:, 1]).reshape(extent_a // 2 * extent_b, extent_c)
    rows = extent_a // 2 * extent_b
    flat = jnp.dot(pair_matrix(rows // 2, rows, 0), flat, precision=lax.Precision.HIGHEST)
    flat = jnp.dot(flat, pair_matrix(extent_c, extent_c // 2, 1), precision=lax.Precision.HIGHEST)
    return flat.reshape(extent_a // 2, extent_b // 2, extent_c // 2) * 0.125


def exchange(stack, width):
    for axis, dim in (("gz", 3), ("gy", 2), ("gx", 1)):
        count = lax.axis_size(axis)
        head = lax.slice_in_dim(stack, 0, width, axis=dim)
        tail = lax.slice_in_dim(stack, stack.shape[dim] - width, stack.shape[dim], axis=dim)
        if count == 2:
            first = lax.axis_index(axis) == 0
            incoming = lax.ppermute(jnp.where(first, tail, head), axis, [(0, 1), (1, 0)])
            nothing = jnp.zeros_like(incoming)
            from_left = jnp.where(first, nothing, incoming)
            from_right = jnp.where(first, incoming, nothing)
        else:
            from_left = lax.ppermute(tail, axis, [(i, i + 1) for i in range(count - 1)])
            from_right = lax.ppermute(head, axis, [(i + 1, i) for i in range(count - 1)])
        stack = jnp.concatenate([from_left, stack, from_right], axis=dim)
    return stack


def inside(shape, width):
    masks = []
    for axis, extent in zip(("gx", "gy", "gz"), shape):
        place = lax.axis_index(axis) * extent - width
        place = place + lax.broadcasted_iota(jnp.int32, (extent + 2 * width,), 0)
        masks.append((place >= 0) & (place < extent * lax.axis_size(axis)))
    return masks[0][:, None, None] & masks[1][None, :, None] & masks[2][None, None, :]


def crop(field, k):
    if k == 0:
        return field
    return field[k:-k, k:-k, k:-k]


def sweep(padded, source, scale):
    centre = padded[1:-1, 1:-1, 1:-1]
    return centre * (1.0 - OMEGA) + (source + neighbours(padded)) * scale


def smooth_wide(start, source, diagonal, mask, steps):
    current = start
    scale = OMEGA / diagonal
    for step in range(1, steps + 1):
        current = sweep(current, crop(source, step), crop(scale, step))
        current = jnp.where(crop(mask, step), current, 0.0)
    return current


def coarser_level(source, damp):
    width = SWEEPS
    wide = exchange(jnp.stack([source, damp]), width)
    wide_source = wide[0]
    wide_diag = 6.0 + wide[1]
    mask = inside(source.shape, width)
    start = jnp.where(mask, OMEGA * wide_source / wide_diag, 0.0)
    current = smooth_wide(start, wide_source, wide_diag, mask, SWEEPS - 1)
    return crop(current, 1), defect(current, source, 6.0 + damp)


def shards(right_side, initial_guess, damping, group_map, block_inverse):
    width = SWEEPS + 1
    wide = exchange(jnp.stack([initial_guess, right_side, damping]), width)
    wide_source = wide[1]
    wide_diag = 6.0 + wide[2]
    mask = inside(right_side.shape, width)
    current = smooth_wide(wide[0], wide_source, wide_diag, mask, SWEEPS)
    iterate = crop(current, 1)
    fine_defect = defect(current, right_side, 6.0 + damping)
    middle_damp = 4.0 * shrink(damping)
    middle_source = 4.0 * shrink(fine_defect)
    middle, middle_defect = coarser_level(middle_source, middle_damp)
    coarse_damp = 4.0 * shrink(middle_damp)
    coarse_source = 4.0 * shrink(middle_defect)
    coarse, coarse_defect = coarser_level(coarse_source, coarse_damp)
    cells = coarse_defect.size
    one_hot = (
        group_map.reshape(cells, 1) == lax.broadcasted_iota(jnp.int32, (cells, NAGG), 1)
    ).astype(jnp.float32)
    partial_sums = jnp.dot(
        coarse_defect.reshape(1, cells), one_hot, precision=lax.Precision.HIGHEST
    ).reshape(NAGG)
    summed = lax.psum(partial_sums, "gz")
    summed = lax.psum(summed, "gx")
    splits = ((1, 2), (2, 2), (4, 4)) if lax.axis_size("gy") == 16 else ((1, lax.axis_size("gy")),)
    for stride, span in splits:
        groups = [
            [base + stride * k for k in range(span)]
            for base in range(lax.axis_size("gy"))
            if base % (stride * span) < stride
        ]
        summed = lax.psum(summed, "gy", axis_index_groups=groups)
    group_cells = (
        coarse_source.size * lax.axis_size("gx") * lax.axis_size("gy") * lax.axis_size("gz") // NAGG
    )
    aggregate_source = summed / math.sqrt(group_cells)
    solution = jnp.dot(block_inverse, aggregate_source, precision=lax.Precision.HIGHEST)
    return (iterate, middle, coarse, solution)


def solution(mesh):
    return jax.shard_map(
        shards,
        mesh=mesh,
        in_specs=(
            P("gx", "gy", "gz"),
            P("gx", "gy", "gz"),
            P("gx", "gy", "gz"),
            P("gx", "gy", "gz"),
            P("gy", None),
        ),
        out_specs=(P("gx", "gy", "gz"), P("gx", "gy", "gz"), P("gx", "gy", "gz"), P("gy")),
        check_vma=False,
    )
```

```python
import math

import jax
import jax.numpy as jnp
from jax import lax
from jax.sharding import PartitionSpec as P

SWEEPS = 4
NAGG = 1024


OMEGA = 0.8


def with_halo(cells, sides, width):
    for axis, dim in sides:
        count = lax.axis_size(axis)
        ends = count - 1
        head = lax.slice_in_dim(cells, 0, width, axis=dim)
        tail = lax.slice_in_dim(cells, cells.shape[dim] - width, cells.shape[dim], axis=dim)
        cells = jnp.concatenate(
            [
                lax.ppermute(tail, axis, [(i, (i + 1) % count) for i in range(ends)]),
                cells,
                lax.ppermute(head, axis, [((i + 1) % count, i) for i in range(ends)]),
            ],
            axis=dim,
        )
    return cells


def neighbours(padded):
    total = padded[2:, 1:-1, 1:-1] + padded[:-2, 1:-1, 1:-1]
    total = total + padded[1:-1, 2:, 1:-1] + padded[1:-1, :-2, 1:-1]
    return total + padded[1:-1, 1:-1, 2:] + padded[1:-1, 1:-1, :-2]


def relax(padded, source, diagonal):
    centre = padded[1:-1, 1:-1, 1:-1]
    return centre + OMEGA * (source - (diagonal * centre - neighbours(padded))) / diagonal


def defect(padded, source, diagonal):
    centre = padded[1:-1, 1:-1, 1:-1]
    return source - (diagonal * centre - neighbours(padded))


def pair_matrix(rows, cols, along):
    row = lax.broadcasted_iota(jnp.int32, (rows, cols), 0)
    col = lax.broadcasted_iota(jnp.int32, (rows, cols), 1)
    if along == 0:
        return (col // 2 == row).astype(jnp.float32)
    return (row // 2 == col).astype(jnp.float32)


def shrink(field):
    extent_a, extent_b, extent_c = field.shape
    halves = field.reshape(extent_a // 2, 2, extent_b, extent_c)
    flat = (halves[:, 0] + halves[:, 1]).reshape(extent_a // 2 * extent_b, extent_c)
    rows = extent_a // 2 * extent_b
    flat = jnp.dot(pair_matrix(rows // 2, rows, 0), flat, precision=lax.Precision.HIGHEST)
    flat = jnp.dot(flat, pair_matrix(extent_c, extent_c // 2, 1), precision=lax.Precision.HIGHEST)
    return flat.reshape(extent_a // 2, extent_b // 2, extent_c // 2) * 0.125


def exchange(stack, width):
    for axis, dim in (("gz", 3), ("gy", 2), ("gx", 1)):
        count = lax.axis_size(axis)
        head = lax.slice_in_dim(stack, 0, width, axis=dim)
        tail = lax.slice_in_dim(stack, stack.shape[dim] - width, stack.shape[dim], axis=dim)
        stack = jnp.concatenate(
            [
                lax.ppermute(tail, axis, [(i, i + 1) for i in range(count - 1)]),
                stack,
                lax.ppermute(head, axis, [(i + 1, i) for i in range(count - 1)]),
            ],
            axis=dim,
        )
    return stack


def inside(shape, width):
    masks = []
    for axis, extent in zip(("gx", "gy", "gz"), shape):
        place = lax.axis_index(axis) * extent - width
        place = place + lax.broadcasted_iota(jnp.int32, (extent + 2 * width,), 0)
        masks.append((place >= 0) & (place < extent * lax.axis_size(axis)))
    return masks[0][:, None, None] & masks[1][None, :, None] & masks[2][None, None, :]


def crop(field, k):
    if k == 0:
        return field
    return field[k:-k, k:-k, k:-k]


def sweep(padded, source, scale):
    centre = padded[1:-1, 1:-1, 1:-1]
    return centre * (1.0 - OMEGA) + (source + neighbours(padded)) * scale


def smooth_wide(start, source, diagonal, mask, steps):
    current = start
    scale = OMEGA / diagonal
    for step in range(1, steps + 1):
        current = sweep(current, crop(source, step), crop(scale, step))
        current = jnp.where(crop(mask, step), current, 0.0)
    return current


def coarser_level(source, damp):
    width = SWEEPS
    wide = exchange(jnp.stack([source, damp]), width)
    wide_source = wide[0]
    wide_diag = 6.0 + wide[1]
    mask = inside(source.shape, width)
    start = jnp.where(mask, OMEGA * wide_source / wide_diag, 0.0)
    current = smooth_wide(start, wide_source, wide_diag, mask, SWEEPS - 1)
    return crop(current, 1), defect(current, source, 6.0 + damp)


def shards(right_side, initial_guess, damping, group_map, block_inverse):
    width = SWEEPS + 1
    wide = exchange(jnp.stack([initial_guess, right_side, damping]), width)
    wide_source = wide[1]
    wide_diag = 6.0 + wide[2]
    mask = inside(right_side.shape, width)
    current = smooth_wide(wide[0], wide_source, wide_diag, mask, SWEEPS)
    iterate = crop(current, 1)
    fine_defect = defect(current, right_side, 6.0 + damping)
    middle_damp = 4.0 * shrink(damping)
    middle_source = 4.0 * shrink(fine_defect)
    middle, middle_defect = coarser_level(middle_source, middle_damp)
    coarse_damp = 4.0 * shrink(middle_damp)
    coarse_source = 4.0 * shrink(middle_defect)
    coarse, coarse_defect = coarser_level(coarse_source, coarse_damp)
    cells = coarse_defect.size
    one_hot = (
        group_map.reshape(cells, 1) == lax.broadcasted_iota(jnp.int32, (cells, NAGG), 1)
    ).astype(jnp.float32)
    partial_sums = jnp.dot(
        coarse_defect.reshape(1, cells), one_hot, precision=lax.Precision.HIGHEST
    ).reshape(NAGG)
    summed = lax.psum(partial_sums, "gz")
    summed = lax.psum(summed, "gx")
    for stride, span in ((1, 2), (2, 2), (4, 4)):
        groups = [
            [base + stride * k for k in range(span)]
            for base in range(lax.axis_size("gy"))
            if base % (stride * span) < stride
        ]
        summed = lax.psum(summed, "gy", axis_index_groups=groups)
    group_cells = (
        coarse_source.size * lax.axis_size("gx") * lax.axis_size("gy") * lax.axis_size("gz") // NAGG
    )
    aggregate_source = summed / math.sqrt(group_cells)
    solution = jnp.dot(block_inverse, aggregate_source, precision=lax.Precision.HIGHEST)
    return (iterate, middle, coarse, solution)


def solution(mesh):
    return jax.shard_map(
        shards,
        mesh=mesh,
        in_specs=(
            P("gx", "gy", "gz"),
            P("gx", "gy", "gz"),
            P("gx", "gy", "gz"),
            P("gx", "gy", "gz"),
            P("gy", None),
        ),
        out_specs=(P("gx", "gy", "gz"), P("gx", "gy", "gz"), P("gx", "gy", "gz"), P("gy")),
        check_vma=False,
    )
```

```python
import math

import jax
import jax.numpy as jnp
from jax import lax
from jax.sharding import PartitionSpec as P

SWEEPS = 4
NAGG = 1024


OMEGA = 0.8


def with_halo(cells, sides, width):
    for axis, dim in sides:
        count = lax.axis_size(axis)
        ends = count - 1
        head = lax.slice_in_dim(cells, 0, width, axis=dim)
        tail = lax.slice_in_dim(cells, cells.shape[dim] - width, cells.shape[dim], axis=dim)
        cells = jnp.concatenate(
            [
                lax.ppermute(tail, axis, [(i, (i + 1) % count) for i in range(ends)]),
                cells,
                lax.ppermute(head, axis, [((i + 1) % count, i) for i in range(ends)]),
            ],
            axis=dim,
        )
    return cells


def neighbours(padded):
    total = padded[2:, 1:-1, 1:-1] + padded[:-2, 1:-1, 1:-1]
    total = total + padded[1:-1, 2:, 1:-1] + padded[1:-1, :-2, 1:-1]
    return total + padded[1:-1, 1:-1, 2:] + padded[1:-1, 1:-1, :-2]


def relax(padded, source, diagonal):
    centre = padded[1:-1, 1:-1, 1:-1]
    return centre + OMEGA * (source - (diagonal * centre - neighbours(padded))) / diagonal


def defect(padded, source, diagonal):
    centre = padded[1:-1, 1:-1, 1:-1]
    return source - (diagonal * centre - neighbours(padded))


def pair_matrix(rows, cols, along):
    row = lax.broadcasted_iota(jnp.int32, (rows, cols), 0)
    col = lax.broadcasted_iota(jnp.int32, (rows, cols), 1)
    if along == 0:
        return (col // 2 == row).astype(jnp.float32)
    return (row // 2 == col).astype(jnp.float32)


def shrink(field):
    extent_a, extent_b, extent_c = field.shape
    halves = field.reshape(extent_a // 2, 2, extent_b, extent_c)
    flat = (halves[:, 0] + halves[:, 1]).reshape(extent_a // 2 * extent_b, extent_c)
    rows = extent_a // 2 * extent_b
    flat = jnp.dot(pair_matrix(rows // 2, rows, 0), flat, precision=lax.Precision.HIGHEST)
    flat = jnp.dot(flat, pair_matrix(extent_c, extent_c // 2, 1), precision=lax.Precision.HIGHEST)
    return flat.reshape(extent_a // 2, extent_b // 2, extent_c // 2) * 0.125


def exchange(stack, width):
    count = lax.axis_size("gz")
    head = lax.slice_in_dim(stack, 0, width, axis=3)
    tail = lax.slice_in_dim(stack, stack.shape[3] - width, stack.shape[3], axis=3)
    stack = jnp.concatenate(
        [
            lax.ppermute(tail, "gz", [(i, i + 1) for i in range(count - 1)]),
            stack,
            lax.ppermute(head, "gz", [(i + 1, i) for i in range(count - 1)]),
        ],
        axis=3,
    )
    rows, cols = lax.axis_size("gx"), lax.axis_size("gy")
    low, high = slice(0, width), slice(-width, None)
    everything = slice(None)

    def shifted(piece, step_x, step_y):
        pairs = [
            (x * cols + y, (x + step_x) * cols + y + step_y)
            for x in range(rows)
            for y in range(cols)
            if 0 <= x + step_x < rows and 0 <= y + step_y < cols
        ]
        if step_x == 0:
            return lax.ppermute(piece, "gy", [(a % cols, b % cols) for a, b in pairs[:cols - 1]])
        if step_y == 0:
            return lax.ppermute(piece, "gx", [(a // cols, b // cols) for a, b in pairs[::cols]])
        return lax.ppermute(piece, ("gx", "gy"), pairs)

    def part(along_x, along_y):
        return stack[:, along_x, along_y]

    band_low = jnp.concatenate(
        [shifted(part(high, high), 1, 1), shifted(part(high, everything), 1, 0), shifted(part(high, low), 1, -1)],
        axis=2,
    )
    band_mid = jnp.concatenate(
        [shifted(part(everything, high), 0, 1), stack, shifted(part(everything, low), 0, -1)],
        axis=2,
    )
    band_high = jnp.concatenate(
        [shifted(part(low, high), -1, 1), shifted(part(low, everything), -1, 0), shifted(part(low, low), -1, -1)],
        axis=2,
    )
    return jnp.concatenate([band_low, band_mid, band_high], axis=1)


def inside(shape, width):
    masks = []
    for axis, extent in zip(("gx", "gy", "gz"), shape):
        place = lax.axis_index(axis) * extent - width
        place = place + lax.broadcasted_iota(jnp.int32, (extent + 2 * width,), 0)
        masks.append((place >= 0) & (place < extent * lax.axis_size(axis)))
    return masks[0][:, None, None] & masks[1][None, :, None] & masks[2][None, None, :]


def crop(field, k):
    if k == 0:
        return field
    return field[k:-k, k:-k, k:-k]


def smooth_wide(start, source, diagonal, mask, steps):
    current = start
    for step in range(1, steps + 1):
        current = relax(current, crop(source, step), crop(diagonal, step))
        current = jnp.where(crop(mask, step), current, 0.0)
    return current


def coarser_level(source, damp):
    width = SWEEPS
    wide = exchange(jnp.stack([source, damp]), width)
    wide_source = wide[0]
    wide_diag = 6.0 + wide[1]
    mask = inside(source.shape, width)
    start = jnp.where(mask, OMEGA * wide_source / wide_diag, 0.0)
    current = smooth_wide(start, wide_source, wide_diag, mask, SWEEPS - 1)
    return crop(current, 1), defect(current, source, 6.0 + damp)


def shards(right_side, initial_guess, damping, group_map, block_inverse):
    width = SWEEPS + 1
    wide = exchange(jnp.stack([initial_guess, right_side, damping]), width)
    wide_source = wide[1]
    wide_diag = 6.0 + wide[2]
    mask = inside(right_side.shape, width)
    current = smooth_wide(wide[0], wide_source, wide_diag, mask, SWEEPS)
    iterate = crop(current, 1)
    fine_defect = defect(current, right_side, 6.0 + damping)
    middle_damp = 4.0 * shrink(damping)
    middle_source = 4.0 * shrink(fine_defect)
    middle, middle_defect = coarser_level(middle_source, middle_damp)
    coarse_damp = 4.0 * shrink(middle_damp)
    coarse_source = 4.0 * shrink(middle_defect)
    coarse, coarse_defect = coarser_level(coarse_source, coarse_damp)
    cells = coarse_defect.size
    one_hot = (
        group_map.reshape(cells, 1) == lax.broadcasted_iota(jnp.int32, (cells, NAGG), 1)
    ).astype(jnp.float32)
    partial_sums = jnp.dot(
        coarse_defect.reshape(1, cells), one_hot, precision=lax.Precision.HIGHEST
    ).reshape(NAGG)
    summed = lax.psum(partial_sums, "gz")
    summed = lax.psum(summed, "gx")
    splits = ((1, 2), (2, 2), (4, 4)) if lax.axis_size("gy") == 16 else ((1, lax.axis_size("gy")),)
    for stride, span in splits:
        groups = [
            [base + stride * k for k in range(span)]
            for base in range(lax.axis_size("gy"))
            if base % (stride * span) < stride
        ]
        summed = lax.psum(summed, "gy", axis_index_groups=groups)
    group_cells = (
        coarse_source.size * lax.axis_size("gx") * lax.axis_size("gy") * lax.axis_size("gz") // NAGG
    )
    aggregate_source = summed / math.sqrt(group_cells)
    solution = jnp.dot(block_inverse, aggregate_source, precision=lax.Precision.HIGHEST)
    return (iterate, middle, coarse, solution)


def solution(mesh):
    return jax.shard_map(
        shards,
        mesh=mesh,
        in_specs=(
            P("gx", "gy", "gz"),
            P("gx", "gy", "gz"),
            P("gx", "gy", "gz"),
            P("gx", "gy", "gz"),
            P("gy", None),
        ),
        out_specs=(P("gx", "gy", "gz"), P("gx", "gy", "gz"), P("gx", "gy", "gz"), P("gy")),
        check_vma=False,
    )
```

```python
import math

import jax
import jax.numpy as jnp
from jax import lax
from jax.sharding import PartitionSpec as P

SWEEPS = 4
NAGG = 1024
DIGITS = 32


OMEGA = 0.8


def with_halo(cells, sides, width):
    for axis, dim in sides:
        count = lax.axis_size(axis)
        ends = count - 1
        head = lax.slice_in_dim(cells, 0, width, axis=dim)
        tail = lax.slice_in_dim(cells, cells.shape[dim] - width, cells.shape[dim], axis=dim)
        cells = jnp.concatenate(
            [
                lax.ppermute(tail, axis, [(i, (i + 1) % count) for i in range(ends)]),
                cells,
                lax.ppermute(head, axis, [((i + 1) % count, i) for i in range(ends)]),
            ],
            axis=dim,
        )
    return cells


def neighbours(padded):
    total = padded[2:, 1:-1, 1:-1] + padded[:-2, 1:-1, 1:-1]
    total = total + padded[1:-1, 2:, 1:-1] + padded[1:-1, :-2, 1:-1]
    return total + padded[1:-1, 1:-1, 2:] + padded[1:-1, 1:-1, :-2]


def relax(padded, source, diagonal):
    centre = padded[1:-1, 1:-1, 1:-1]
    return centre + OMEGA * (source - (diagonal * centre - neighbours(padded))) / diagonal


def defect(padded, source, diagonal):
    centre = padded[1:-1, 1:-1, 1:-1]
    return source - (diagonal * centre - neighbours(padded))


def pair_matrix(rows, cols, along):
    row = lax.broadcasted_iota(jnp.int32, (rows, cols), 0)
    col = lax.broadcasted_iota(jnp.int32, (rows, cols), 1)
    if along == 0:
        return (col // 2 == row).astype(jnp.float32)
    return (row // 2 == col).astype(jnp.float32)


def shrink(field):
    extent_a, extent_b, extent_c = field.shape
    halves = field.reshape(extent_a // 2, 2, extent_b, extent_c)
    flat = (halves[:, 0] + halves[:, 1]).reshape(extent_a // 2 * extent_b, extent_c)
    rows = extent_a // 2 * extent_b
    flat = jnp.dot(pair_matrix(rows // 2, rows, 0), flat, precision=lax.Precision.HIGHEST)
    flat = jnp.dot(flat, pair_matrix(extent_c, extent_c // 2, 1), precision=lax.Precision.HIGHEST)
    return flat.reshape(extent_a // 2, extent_b // 2, extent_c // 2) * 0.125


def exchange(stack, width):
    for axis, dim in (("gz", 3), ("gy", 2), ("gx", 1)):
        count = lax.axis_size(axis)
        head = lax.slice_in_dim(stack, 0, width, axis=dim)
        tail = lax.slice_in_dim(stack, stack.shape[dim] - width, stack.shape[dim], axis=dim)
        stack = jnp.concatenate(
            [
                lax.ppermute(tail, axis, [(i, i + 1) for i in range(count - 1)]),
                stack,
                lax.ppermute(head, axis, [(i + 1, i) for i in range(count - 1)]),
            ],
            axis=dim,
        )
    return stack


def inside(shape, width):
    masks = []
    for axis, extent in zip(("gx", "gy", "gz"), shape):
        place = lax.axis_index(axis) * extent - width
        place = place + lax.broadcasted_iota(jnp.int32, (extent + 2 * width,), 0)
        masks.append((place >= 0) & (place < extent * lax.axis_size(axis)))
    return masks[0][:, None, None] & masks[1][None, :, None] & masks[2][None, None, :]


def crop(field, k):
    if k == 0:
        return field
    return field[k:-k, k:-k, k:-k]


def smooth_wide(start, source, diagonal, mask, steps):
    current = start
    for step in range(1, steps + 1):
        current = relax(current, crop(source, step), crop(diagonal, step))
        current = jnp.where(crop(mask, step), current, 0.0)
    return current


def coarser_level(source, damp):
    width = SWEEPS
    wide = exchange(jnp.stack([source, damp]), width)
    wide_source = wide[0]
    wide_diag = 6.0 + wide[1]
    mask = inside(source.shape, width)
    start = jnp.where(mask, OMEGA * wide_source / wide_diag, 0.0)
    current = smooth_wide(start, wide_source, wide_diag, mask, SWEEPS - 1)
    return crop(current, 1), defect(current, source, 6.0 + damp)


def shards(right_side, initial_guess, damping, group_map, block_inverse):
    width = SWEEPS + 1
    wide = exchange(jnp.stack([initial_guess, right_side, damping]), width)
    wide_source = wide[1]
    wide_diag = 6.0 + wide[2]
    mask = inside(right_side.shape, width)
    current = smooth_wide(wide[0], wide_source, wide_diag, mask, SWEEPS)
    iterate = crop(current, 1)
    fine_defect = defect(current, right_side, 6.0 + damping)
    middle_damp = 4.0 * shrink(damping)
    middle_source = 4.0 * shrink(fine_defect)
    middle, middle_defect = coarser_level(middle_source, middle_damp)
    coarse_damp = 4.0 * shrink(middle_damp)
    coarse_source = 4.0 * shrink(middle_defect)
    coarse, coarse_defect = coarser_level(coarse_source, coarse_damp)
    cells = coarse_defect.size
    digits = DIGITS
    owner = group_map.reshape(cells, 1)
    letters = lax.broadcasted_iota(jnp.int32, (cells, digits), 1)
    high = (owner // digits == letters).astype(jnp.float32) * coarse_defect.reshape(cells, 1)
    low = (owner % digits == letters).astype(jnp.float32)
    partial_sums = lax.dot_general(
        high, low, (((0,), (0,)), ((), ())), precision=lax.Precision.HIGHEST
    ).reshape(NAGG)
    summed = lax.psum(partial_sums, "gz")
    summed = lax.psum(summed, "gx")
    splits = ((1, 2), (2, 2), (4, 4)) if lax.axis_size("gy") == 16 else ((1, lax.axis_size("gy")),)
    for stride, span in splits:
        groups = [
            [base + stride * k for k in range(span)]
            for base in range(lax.axis_size("gy"))
            if base % (stride * span) < stride
        ]
        summed = lax.psum(summed, "gy", axis_index_groups=groups)
    group_cells = (
        coarse_source.size * lax.axis_size("gx") * lax.axis_size("gy") * lax.axis_size("gz") // NAGG
    )
    aggregate_source = summed / math.sqrt(group_cells)
    solution = jnp.dot(block_inverse, aggregate_source, precision=lax.Precision.HIGHEST)
    return (iterate, middle, coarse, solution)


def solution(mesh):
    return jax.shard_map(
        shards,
        mesh=mesh,
        in_specs=(
            P("gx", "gy", "gz"),
            P("gx", "gy", "gz"),
            P("gx", "gy", "gz"),
            P("gx", "gy", "gz"),
            P("gy", None),
        ),
        out_specs=(P("gx", "gy", "gz"), P("gx", "gy", "gz"), P("gx", "gy", "gz"), P("gy")),
        check_vma=False,
    )
```

```python
import math

import jax
import jax.numpy as jnp
from jax import lax
from jax.sharding import PartitionSpec as P

SWEEPS = 4
NAGG = 1024
DIGITS = 32


OMEGA = 0.8


def with_halo(cells, sides, width):
    for axis, dim in sides:
        count = lax.axis_size(axis)
        ends = count - 1
        head = lax.slice_in_dim(cells, 0, width, axis=dim)
        tail = lax.slice_in_dim(cells, cells.shape[dim] - width, cells.shape[dim], axis=dim)
        cells = jnp.concatenate(
            [
                lax.ppermute(tail, axis, [(i, (i + 1) % count) for i in range(ends)]),
                cells,
                lax.ppermute(head, axis, [((i + 1) % count, i) for i in range(ends)]),
            ],
            axis=dim,
        )
    return cells


def neighbours(padded):
    total = padded[2:, 1:-1, 1:-1] + padded[:-2, 1:-1, 1:-1]
    total = total + padded[1:-1, 2:, 1:-1] + padded[1:-1, :-2, 1:-1]
    return total + padded[1:-1, 1:-1, 2:] + padded[1:-1, 1:-1, :-2]


def relax(padded, source, diagonal):
    centre = padded[1:-1, 1:-1, 1:-1]
    return centre + OMEGA * (source - (diagonal * centre - neighbours(padded))) / diagonal


def defect(padded, source, diagonal):
    centre = padded[1:-1, 1:-1, 1:-1]
    return source - (diagonal * centre - neighbours(padded))


def pair_matrix(rows, cols, along):
    row = lax.broadcasted_iota(jnp.int32, (rows, cols), 0)
    col = lax.broadcasted_iota(jnp.int32, (rows, cols), 1)
    if along == 0:
        return (col // 2 == row).astype(jnp.float32)
    return (row // 2 == col).astype(jnp.float32)


def shrink(field):
    extent_a, extent_b, extent_c = field.shape
    halves = field.reshape(extent_a // 2, 2, extent_b, extent_c)
    flat = (halves[:, 0] + halves[:, 1]).reshape(extent_a // 2 * extent_b, extent_c)
    rows = extent_a // 2 * extent_b
    flat = jnp.dot(pair_matrix(rows // 2, rows, 0), flat, precision=lax.Precision.HIGHEST)
    flat = jnp.dot(flat, pair_matrix(extent_c, extent_c // 2, 1), precision=lax.Precision.HIGHEST)
    return flat.reshape(extent_a // 2, extent_b // 2, extent_c // 2) * 0.125


def exchange(stack, width):
    for axis, dim in (("gx", 1), ("gy", 2), ("gz", 3)):
        count = lax.axis_size(axis)
        head = lax.slice_in_dim(stack, 0, width, axis=dim)
        tail = lax.slice_in_dim(stack, stack.shape[dim] - width, stack.shape[dim], axis=dim)
        stack = jnp.concatenate(
            [
                lax.ppermute(tail, axis, [(i, i + 1) for i in range(count - 1)]),
                stack,
                lax.ppermute(head, axis, [(i + 1, i) for i in range(count - 1)]),
            ],
            axis=dim,
        )
    return stack


def inside(shape, width):
    masks = []
    for axis, extent in zip(("gx", "gy", "gz"), shape):
        place = lax.axis_index(axis) * extent - width
        place = place + lax.broadcasted_iota(jnp.int32, (extent + 2 * width,), 0)
        masks.append((place >= 0) & (place < extent * lax.axis_size(axis)))
    return masks[0][:, None, None] & masks[1][None, :, None] & masks[2][None, None, :]


def crop(field, k):
    if k == 0:
        return field
    return field[k:-k, k:-k, k:-k]


def smooth_wide(start, source, diagonal, mask, steps):
    current = start
    for step in range(1, steps + 1):
        current = relax(current, crop(source, step), crop(diagonal, step))
        current = jnp.where(crop(mask, step), current, 0.0)
    return current


def coarser_level(source, damp):
    width = SWEEPS
    wide = exchange(jnp.stack([source, damp]), width)
    wide_source = wide[0]
    wide_diag = 6.0 + wide[1]
    mask = inside(source.shape, width)
    start = jnp.where(mask, OMEGA * wide_source / wide_diag, 0.0)
    current = smooth_wide(start, wide_source, wide_diag, mask, SWEEPS - 1)
    return crop(current, 1), defect(current, source, 6.0 + damp)


def shards(right_side, initial_guess, damping, group_map, block_inverse):
    width = SWEEPS + 1
    wide = exchange(jnp.stack([initial_guess, right_side, damping]), width)
    wide_source = wide[1]
    wide_diag = 6.0 + wide[2]
    mask = inside(right_side.shape, width)
    current = smooth_wide(wide[0], wide_source, wide_diag, mask, SWEEPS)
    iterate = crop(current, 1)
    fine_defect = defect(current, right_side, 6.0 + damping)
    middle_damp = 4.0 * shrink(damping)
    middle_source = 4.0 * shrink(fine_defect)
    middle, middle_defect = coarser_level(middle_source, middle_damp)
    coarse_damp = 4.0 * shrink(middle_damp)
    coarse_source = 4.0 * shrink(middle_defect)
    coarse, coarse_defect = coarser_level(coarse_source, coarse_damp)
    cells = coarse_defect.size
    digits = DIGITS
    owner = group_map.reshape(cells, 1)
    letters = lax.broadcasted_iota(jnp.int32, (cells, digits), 1)
    high = (owner // digits == letters).astype(jnp.float32) * coarse_defect.reshape(cells, 1)
    low = (owner % digits == letters).astype(jnp.float32)
    partial_sums = lax.dot_general(
        high, low, (((0,), (0,)), ((), ())), precision=lax.Precision.HIGHEST
    ).reshape(NAGG)
    summed = lax.psum(partial_sums, "gz")
    summed = lax.psum(summed, "gx")
    splits = ((1, 2), (2, 2), (4, 4)) if lax.axis_size("gy") == 16 else ((1, lax.axis_size("gy")),)
    for stride, span in splits:
        groups = [
            [base + stride * k for k in range(span)]
            for base in range(lax.axis_size("gy"))
            if base % (stride * span) < stride
        ]
        summed = lax.psum(summed, "gy", axis_index_groups=groups)
    group_cells = (
        coarse_source.size * lax.axis_size("gx") * lax.axis_size("gy") * lax.axis_size("gz") // NAGG
    )
    aggregate_source = summed / math.sqrt(group_cells)
    solution = jnp.dot(block_inverse, aggregate_source, precision=lax.Precision.HIGHEST)
    return (iterate, middle, coarse, solution)


def solution(mesh):
    return jax.shard_map(
        shards,
        mesh=mesh,
        in_specs=(
            P("gx", "gy", "gz"),
            P("gx", "gy", "gz"),
            P("gx", "gy", "gz"),
            P("gx", "gy", "gz"),
            P("gy", None),
        ),
        out_specs=(P("gx", "gy", "gz"), P("gx", "gy", "gz"), P("gx", "gy", "gz"), P("gy")),
        check_vma=False,
    )
```

```python
import math

import jax
import jax.numpy as jnp
from jax import lax
from jax.sharding import PartitionSpec as P

SWEEPS = 4
NAGG = 1024
DIGITS = 32


OMEGA = 0.8


def with_halo(cells, sides, width):
    for axis, dim in sides:
        count = lax.axis_size(axis)
        ends = count - 1
        head = lax.slice_in_dim(cells, 0, width, axis=dim)
        tail = lax.slice_in_dim(cells, cells.shape[dim] - width, cells.shape[dim], axis=dim)
        cells = jnp.concatenate(
            [
                lax.ppermute(tail, axis, [(i, (i + 1) % count) for i in range(ends)]),
                cells,
                lax.ppermute(head, axis, [((i + 1) % count, i) for i in range(ends)]),
            ],
            axis=dim,
        )
    return cells


def neighbours(padded):
    total = padded[2:, 1:-1, 1:-1] + padded[:-2, 1:-1, 1:-1]
    total = total + padded[1:-1, 2:, 1:-1] + padded[1:-1, :-2, 1:-1]
    return total + padded[1:-1, 1:-1, 2:] + padded[1:-1, 1:-1, :-2]


def relax(padded, source, diagonal):
    centre = padded[1:-1, 1:-1, 1:-1]
    return centre + OMEGA * (source - (diagonal * centre - neighbours(padded))) / diagonal


def defect(padded, source, diagonal):
    centre = padded[1:-1, 1:-1, 1:-1]
    return source - (diagonal * centre - neighbours(padded))


def pair_matrix(rows, cols, along):
    row = lax.broadcasted_iota(jnp.int32, (rows, cols), 0)
    col = lax.broadcasted_iota(jnp.int32, (rows, cols), 1)
    if along == 0:
        return (col // 2 == row).astype(jnp.float32)
    return (row // 2 == col).astype(jnp.float32)


def shrink(field):
    extent_a, extent_b, extent_c = field.shape
    halves = field.reshape(extent_a // 2, 2, extent_b, extent_c)
    flat = (halves[:, 0] + halves[:, 1]).reshape(extent_a // 2 * extent_b, extent_c)
    rows = extent_a // 2 * extent_b
    flat = jnp.dot(pair_matrix(rows // 2, rows, 0), flat, precision=lax.Precision.HIGHEST)
    flat = jnp.dot(flat, pair_matrix(extent_c, extent_c // 2, 1), precision=lax.Precision.HIGHEST)
    return flat.reshape(extent_a // 2, extent_b // 2, extent_c // 2) * 0.125


def exchange(stack, width):
    for axis, dim in (("gz", 3), ("gx", 1), ("gy", 2)):
        count = lax.axis_size(axis)
        head = lax.slice_in_dim(stack, 0, width, axis=dim)
        tail = lax.slice_in_dim(stack, stack.shape[dim] - width, stack.shape[dim], axis=dim)
        stack = jnp.concatenate(
            [
                lax.ppermute(tail, axis, [(i, i + 1) for i in range(count - 1)]),
                stack,
                lax.ppermute(head, axis, [(i + 1, i) for i in range(count - 1)]),
            ],
            axis=dim,
        )
    return stack


def inside(shape, width):
    masks = []
    for axis, extent in zip(("gx", "gy", "gz"), shape):
        place = lax.axis_index(axis) * extent - width
        place = place + lax.broadcasted_iota(jnp.int32, (extent + 2 * width,), 0)
        masks.append((place >= 0) & (place < extent * lax.axis_size(axis)))
    return masks[0][:, None, None] & masks[1][None, :, None] & masks[2][None, None, :]


def crop(field, k):
    if k == 0:
        return field
    return field[k:-k, k:-k, k:-k]


def smooth_wide(start, source, diagonal, mask, steps):
    current = start
    for step in range(1, steps + 1):
        current = relax(current, crop(source, step), crop(diagonal, step))
        current = jnp.where(crop(mask, step), current, 0.0)
    return current


def coarser_level(source, damp):
    width = SWEEPS
    wide = exchange(jnp.stack([source, damp]), width)
    wide_source = wide[0]
    wide_diag = 6.0 + wide[1]
    mask = inside(source.shape, width)
    start = jnp.where(mask, OMEGA * wide_source / wide_diag, 0.0)
    current = smooth_wide(start, wide_source, wide_diag, mask, SWEEPS - 1)
    return crop(current, 1), defect(current, source, 6.0 + damp)


def shards(right_side, initial_guess, damping, group_map, block_inverse):
    width = SWEEPS + 1
    wide = exchange(jnp.stack([initial_guess, right_side, damping]), width)
    wide_source = wide[1]
    wide_diag = 6.0 + wide[2]
    mask = inside(right_side.shape, width)
    current = smooth_wide(wide[0], wide_source, wide_diag, mask, SWEEPS)
    iterate = crop(current, 1)
    fine_defect = defect(current, right_side, 6.0 + damping)
    middle_damp = 4.0 * shrink(damping)
    middle_source = 4.0 * shrink(fine_defect)
    middle, middle_defect = coarser_level(middle_source, middle_damp)
    coarse_damp = 4.0 * shrink(middle_damp)
    coarse_source = 4.0 * shrink(middle_defect)
    coarse, coarse_defect = coarser_level(coarse_source, coarse_damp)
    cells = coarse_defect.size
    digits = DIGITS
    owner = group_map.reshape(cells, 1)
    letters = lax.broadcasted_iota(jnp.int32, (cells, digits), 1)
    high = (owner // digits == letters).astype(jnp.float32) * coarse_defect.reshape(cells, 1)
    low = (owner % digits == letters).astype(jnp.float32)
    partial_sums = lax.dot_general(
        high, low, (((0,), (0,)), ((), ())), precision=lax.Precision.HIGHEST
    ).reshape(NAGG)
    summed = lax.psum(partial_sums, "gz")
    summed = lax.psum(summed, "gx")
    splits = ((1, 2), (2, 2), (4, 4)) if lax.axis_size("gy") == 16 else ((1, lax.axis_size("gy")),)
    for stride, span in splits:
        groups = [
            [base + stride * k for k in range(span)]
            for base in range(lax.axis_size("gy"))
            if base % (stride * span) < stride
        ]
        summed = lax.psum(summed, "gy", axis_index_groups=groups)
    group_cells = (
        coarse_source.size * lax.axis_size("gx") * lax.axis_size("gy") * lax.axis_size("gz") // NAGG
    )
    aggregate_source = summed / math.sqrt(group_cells)
    solution = jnp.dot(block_inverse, aggregate_source, precision=lax.Precision.HIGHEST)
    return (iterate, middle, coarse, solution)


def solution(mesh):
    return jax.shard_map(
        shards,
        mesh=mesh,
        in_specs=(
            P("gx", "gy", "gz"),
            P("gx", "gy", "gz"),
            P("gx", "gy", "gz"),
            P("gx", "gy", "gz"),
            P("gy", None),
        ),
        out_specs=(P("gx", "gy", "gz"), P("gx", "gy", "gz"), P("gx", "gy", "gz"), P("gy")),
        check_vma=False,
    )
```

```python
import math

import jax
import jax.numpy as jnp
from jax import lax
from jax.sharding import PartitionSpec as P

SWEEPS = 4
NAGG = 1024
DIGITS = 32


OMEGA = 0.8


def with_halo(cells, sides, width):
    for axis, dim in sides:
        count = lax.axis_size(axis)
        ends = count - 1
        head = lax.slice_in_dim(cells, 0, width, axis=dim)
        tail = lax.slice_in_dim(cells, cells.shape[dim] - width, cells.shape[dim], axis=dim)
        cells = jnp.concatenate(
            [
                lax.ppermute(tail, axis, [(i, (i + 1) % count) for i in range(ends)]),
                cells,
                lax.ppermute(head, axis, [((i + 1) % count, i) for i in range(ends)]),
            ],
            axis=dim,
        )
    return cells


def neighbours(padded):
    total = padded[2:, 1:-1, 1:-1] + padded[:-2, 1:-1, 1:-1]
    total = total + padded[1:-1, 2:, 1:-1] + padded[1:-1, :-2, 1:-1]
    return total + padded[1:-1, 1:-1, 2:] + padded[1:-1, 1:-1, :-2]


def relax(padded, source, diagonal):
    centre = padded[1:-1, 1:-1, 1:-1]
    return centre + OMEGA * (source - (diagonal * centre - neighbours(padded))) / diagonal


def defect(padded, source, diagonal):
    centre = padded[1:-1, 1:-1, 1:-1]
    return source - (diagonal * centre - neighbours(padded))


def pair_matrix(rows, cols, along):
    row = lax.broadcasted_iota(jnp.int32, (rows, cols), 0)
    col = lax.broadcasted_iota(jnp.int32, (rows, cols), 1)
    if along == 0:
        return (col // 2 == row).astype(jnp.float32)
    return (row // 2 == col).astype(jnp.float32)


def shrink(field):
    extent_a, extent_b, extent_c = field.shape
    halves = field.reshape(extent_a // 2, 2, extent_b, extent_c)
    flat = (halves[:, 0] + halves[:, 1]).reshape(extent_a // 2 * extent_b, extent_c)
    rows = extent_a // 2 * extent_b
    flat = jnp.dot(pair_matrix(rows // 2, rows, 0), flat, precision=lax.Precision.HIGHEST)
    flat = jnp.dot(flat, pair_matrix(extent_c, extent_c // 2, 1), precision=lax.Precision.HIGHEST)
    return flat.reshape(extent_a // 2, extent_b // 2, extent_c // 2) * 0.125


def exchange(stack, width):
    for axis, dim in (("gx", 1), ("gy", 2), ("gz", 3)):
        count = lax.axis_size(axis)
        head = lax.slice_in_dim(stack, 0, width, axis=dim)
        tail = lax.slice_in_dim(stack, stack.shape[dim] - width, stack.shape[dim], axis=dim)
        stack = jnp.concatenate(
            [
                lax.ppermute(tail, axis, [(i, i + 1) for i in range(count - 1)]),
                stack,
                lax.ppermute(head, axis, [(i + 1, i) for i in range(count - 1)]),
            ],
            axis=dim,
        )
    return stack


def inside(shape, width):
    masks = []
    for axis, extent in zip(("gx", "gy", "gz"), shape):
        place = lax.axis_index(axis) * extent - width
        place = place + lax.broadcasted_iota(jnp.int32, (extent + 2 * width,), 0)
        masks.append((place >= 0) & (place < extent * lax.axis_size(axis)))
    return masks[0][:, None, None] & masks[1][None, :, None] & masks[2][None, None, :]


def crop(field, k):
    if k == 0:
        return field
    return field[k:-k, k:-k, k:-k]


def smooth_wide(start, source, diagonal, mask, steps):
    current = start
    for step in range(1, steps + 1):
        current = relax(current, crop(source, step), crop(diagonal, step))
        current = jnp.where(crop(mask, step), current, 0.0)
    return current


def coarser_level(source, damp):
    width = SWEEPS
    wide = exchange(jnp.stack([source, damp]), width)
    wide_source = wide[0]
    wide_diag = 6.0 + wide[1]
    mask = inside(source.shape, width)
    start = jnp.where(mask, OMEGA * wide_source / wide_diag, 0.0)
    current = smooth_wide(start, wide_source, wide_diag, mask, SWEEPS - 1)
    return crop(current, 1), defect(current, source, 6.0 + damp)


def shards(right_side, initial_guess, damping, group_map, block_inverse):
    width = SWEEPS + 1
    wide = exchange(jnp.stack([initial_guess, right_side, damping]), width)
    wide_source = wide[1]
    wide_diag = 6.0 + wide[2]
    mask = inside(right_side.shape, width)
    current = smooth_wide(wide[0], wide_source, wide_diag, mask, SWEEPS)
    iterate = crop(current, 1)
    fine_defect = defect(current, right_side, 6.0 + damping)
    middle_damp = 4.0 * shrink(damping)
    middle_source = 4.0 * shrink(fine_defect)
    middle, middle_defect = coarser_level(middle_source, middle_damp)
    coarse_damp = 4.0 * shrink(middle_damp)
    coarse_source = 4.0 * shrink(middle_defect)
    coarse, coarse_defect = coarser_level(coarse_source, coarse_damp)
    cells = coarse_defect.size
    digits = DIGITS
    owner = group_map.reshape(cells, 1)
    letters = lax.broadcasted_iota(jnp.int32, (cells, digits), 1)
    high = (owner // digits == letters).astype(jnp.float32) * coarse_defect.reshape(cells, 1)
    low = (owner % digits == letters).astype(jnp.float32)
    partial_sums = lax.dot_general(
        high, low, (((0,), (0,)), ((), ())), precision=lax.Precision.HIGHEST
    ).reshape(NAGG)
    summed = lax.psum(partial_sums, ("gx", "gz"))
    splits = ((1, 4), (4, 4)) if lax.axis_size("gy") == 16 else ((1, lax.axis_size("gy")),)
    for stride, span in splits:
        groups = [
            [base + stride * k for k in range(span)]
            for base in range(lax.axis_size("gy"))
            if base % (stride * span) < stride
        ]
        summed = lax.psum(summed, "gy", axis_index_groups=groups)
    group_cells = (
        coarse_source.size * lax.axis_size("gx") * lax.axis_size("gy") * lax.axis_size("gz") // NAGG
    )
    aggregate_source = summed / math.sqrt(group_cells)
    solution = jnp.dot(block_inverse, aggregate_source, precision=lax.Precision.HIGHEST)
    return (iterate, middle, coarse, solution)


def solution(mesh):
    return jax.shard_map(
        shards,
        mesh=mesh,
        in_specs=(
            P("gx", "gy", "gz"),
            P("gx", "gy", "gz"),
            P("gx", "gy", "gz"),
            P("gx", "gy", "gz"),
            P("gy", None),
        ),
        out_specs=(P("gx", "gy", "gz"), P("gx", "gy", "gz"), P("gx", "gy", "gz"), P("gy")),
        check_vma=False,
    )
```

```python
import math

import jax
import jax.numpy as jnp
from jax import lax
from jax.sharding import PartitionSpec as P

SWEEPS = 4
NAGG = 1024
DIGITS = 32


OMEGA = 0.8


def with_halo(cells, sides, width):
    for axis, dim in sides:
        count = lax.axis_size(axis)
        ends = count - 1
        head = lax.slice_in_dim(cells, 0, width, axis=dim)
        tail = lax.slice_in_dim(cells, cells.shape[dim] - width, cells.shape[dim], axis=dim)
        cells = jnp.concatenate(
            [
                lax.ppermute(tail, axis, [(i, (i + 1) % count) for i in range(ends)]),
                cells,
                lax.ppermute(head, axis, [((i + 1) % count, i) for i in range(ends)]),
            ],
            axis=dim,
        )
    return cells


def neighbours(padded):
    total = padded[2:, 1:-1, 1:-1] + padded[:-2, 1:-1, 1:-1]
    total = total + padded[1:-1, 2:, 1:-1] + padded[1:-1, :-2, 1:-1]
    return total + padded[1:-1, 1:-1, 2:] + padded[1:-1, 1:-1, :-2]


def relax(padded, source, diagonal):
    centre = padded[1:-1, 1:-1, 1:-1]
    return centre + OMEGA * (source - (diagonal * centre - neighbours(padded))) / diagonal


def defect(padded, source, diagonal):
    centre = padded[1:-1, 1:-1, 1:-1]
    return source - (diagonal * centre - neighbours(padded))


def pair_matrix(rows, cols, along):
    row = lax.broadcasted_iota(jnp.int32, (rows, cols), 0)
    col = lax.broadcasted_iota(jnp.int32, (rows, cols), 1)
    if along == 0:
        return (col // 2 == row).astype(jnp.float32)
    return (row // 2 == col).astype(jnp.float32)


def shrink(field):
    extent_a, extent_b, extent_c = field.shape
    halves = field.reshape(extent_a // 2, 2, extent_b, extent_c)
    flat = (halves[:, 0] + halves[:, 1]).reshape(extent_a // 2 * extent_b, extent_c)
    rows = extent_a // 2 * extent_b
    flat = jnp.dot(pair_matrix(rows // 2, rows, 0), flat, precision=lax.Precision.HIGHEST)
    flat = jnp.dot(flat, pair_matrix(extent_c, extent_c // 2, 1), precision=lax.Precision.HIGHEST)
    return flat.reshape(extent_a // 2, extent_b // 2, extent_c // 2) * 0.125


def exchange(stack, width):
    for axis, dim in (("gx", 1), ("gy", 2), ("gz", 3)):
        count = lax.axis_size(axis)
        head = lax.slice_in_dim(stack, 0, width, axis=dim)
        tail = lax.slice_in_dim(stack, stack.shape[dim] - width, stack.shape[dim], axis=dim)
        stack = jnp.concatenate(
            [
                lax.ppermute(tail, axis, [(i, i + 1) for i in range(count - 1)]),
                stack,
                lax.ppermute(head, axis, [(i + 1, i) for i in range(count - 1)]),
            ],
            axis=dim,
        )
    return stack


def inside(shape, width):
    masks = []
    for axis, extent in zip(("gx", "gy", "gz"), shape):
        place = lax.axis_index(axis) * extent - width
        place = place + lax.broadcasted_iota(jnp.int32, (extent + 2 * width,), 0)
        masks.append((place >= 0) & (place < extent * lax.axis_size(axis)))
    return masks[0][:, None, None] & masks[1][None, :, None] & masks[2][None, None, :]


def crop(field, k):
    if k == 0:
        return field
    return field[k:-k, k:-k, k:-k]


def smooth_wide(start, source, diagonal, mask, steps):
    current = start
    for step in range(1, steps + 1):
        current = relax(current, crop(source, step), crop(diagonal, step))
        current = jnp.where(crop(mask, step), current, 0.0)
    return current


def coarser_level(source, damp):
    width = SWEEPS
    wide = exchange(jnp.stack([source, damp]), width)
    wide_source = wide[0]
    wide_diag = 6.0 + wide[1]
    mask = inside(source.shape, width)
    start = jnp.where(mask, OMEGA * wide_source / wide_diag, 0.0)
    current = smooth_wide(start, wide_source, wide_diag, mask, SWEEPS - 1)
    return crop(current, 1), defect(current, source, 6.0 + damp)


def shards(right_side, initial_guess, damping, group_map, block_inverse):
    width = SWEEPS + 1
    wide = exchange(jnp.stack([initial_guess, right_side, damping]), width)
    wide_source = wide[1]
    wide_diag = 6.0 + wide[2]
    mask = inside(right_side.shape, width)
    current = smooth_wide(wide[0], wide_source, wide_diag, mask, SWEEPS)
    iterate = crop(current, 1)
    fine_defect = defect(current, right_side, 6.0 + damping)
    middle_damp = 4.0 * shrink(damping)
    middle_source = 4.0 * shrink(fine_defect)
    middle, middle_defect = coarser_level(middle_source, middle_damp)
    coarse_damp = 4.0 * shrink(middle_damp)
    coarse_source = 4.0 * shrink(middle_defect)
    coarse, coarse_defect = coarser_level(coarse_source, coarse_damp)
    cells = coarse_defect.size
    digits = DIGITS
    owner = group_map.reshape(cells, 1)
    letters = lax.broadcasted_iota(jnp.int32, (cells, digits), 1)
    high = (owner // digits == letters).astype(jnp.float32) * coarse_defect.reshape(cells, 1)
    low = (owner % digits == letters).astype(jnp.float32)
    partial_sums = lax.dot_general(
        high, low, (((0,), (0,)), ((), ())), precision=lax.Precision.HIGHEST
    ).reshape(NAGG)
    summed = lax.psum(partial_sums, "gz")
    summed = lax.psum(summed, "gx")
    splits = ((1, 4), (4, 4)) if lax.axis_size("gy") == 16 else ((1, lax.axis_size("gy")),)
    for stride, span in splits:
        groups = [
            [base + stride * k for k in range(span)]
            for base in range(lax.axis_size("gy"))
            if base % (stride * span) < stride
        ]
        summed = lax.psum(summed, "gy", axis_index_groups=groups)
    group_cells = (
        coarse_source.size * lax.axis_size("gx") * lax.axis_size("gy") * lax.axis_size("gz") // NAGG
    )
    aggregate_source = summed / math.sqrt(group_cells)
    solution = jnp.dot(block_inverse, aggregate_source, precision=lax.Precision.HIGHEST)
    return (iterate, middle, coarse, solution)


def solution(mesh):
    return jax.shard_map(
        shards,
        mesh=mesh,
        in_specs=(
            P("gx", "gy", "gz"),
            P("gx", "gy", "gz"),
            P("gx", "gy", "gz"),
            P("gx", "gy", "gz"),
            P("gy", None),
        ),
        out_specs=(P("gx", "gy", "gz"), P("gx", "gy", "gz"), P("gx", "gy", "gz"), P("gy")),
        check_vma=False,
    )
```

```python
import math

import jax
import jax.numpy as jnp
from jax import lax
from jax.sharding import PartitionSpec as P

SWEEPS = 4
NAGG = 1024
DIGITS = 32


OMEGA = 0.8


def with_halo(cells, sides, width):
    for axis, dim in sides:
        count = lax.axis_size(axis)
        ends = count - 1
        head = lax.slice_in_dim(cells, 0, width, axis=dim)
        tail = lax.slice_in_dim(cells, cells.shape[dim] - width, cells.shape[dim], axis=dim)
        cells = jnp.concatenate(
            [
                lax.ppermute(tail, axis, [(i, (i + 1) % count) for i in range(ends)]),
                cells,
                lax.ppermute(head, axis, [((i + 1) % count, i) for i in range(ends)]),
            ],
            axis=dim,
        )
    return cells


def neighbours(padded):
    total = padded[2:, 1:-1, 1:-1] + padded[:-2, 1:-1, 1:-1]
    total = total + padded[1:-1, 2:, 1:-1] + padded[1:-1, :-2, 1:-1]
    return total + padded[1:-1, 1:-1, 2:] + padded[1:-1, 1:-1, :-2]


def relax(padded, source, diagonal):
    centre = padded[1:-1, 1:-1, 1:-1]
    return centre + OMEGA * (source - (diagonal * centre - neighbours(padded))) / diagonal


def defect(padded, source, diagonal):
    centre = padded[1:-1, 1:-1, 1:-1]
    return source - (diagonal * centre - neighbours(padded))


def pair_matrix(rows, cols, along):
    row = lax.broadcasted_iota(jnp.int32, (rows, cols), 0)
    col = lax.broadcasted_iota(jnp.int32, (rows, cols), 1)
    if along == 0:
        return (col // 2 == row).astype(jnp.float32)
    return (row // 2 == col).astype(jnp.float32)


def shrink(field):
    extent_a, extent_b, extent_c = field.shape
    halves = field.reshape(extent_a // 2, 2, extent_b, extent_c)
    flat = (halves[:, 0] + halves[:, 1]).reshape(extent_a // 2 * extent_b, extent_c)
    rows = extent_a // 2 * extent_b
    flat = jnp.dot(pair_matrix(rows // 2, rows, 0), flat, precision=lax.Precision.HIGHEST)
    flat = jnp.dot(flat, pair_matrix(extent_c, extent_c // 2, 1), precision=lax.Precision.HIGHEST)
    return flat.reshape(extent_a // 2, extent_b // 2, extent_c // 2) * 0.125


def exchange(stack, width, swap=False):
    for axis, dim in (("gx", 1), ("gy", 2), ("gz", 3)):
        count = lax.axis_size(axis)
        head = lax.slice_in_dim(stack, 0, width, axis=dim)
        tail = lax.slice_in_dim(stack, stack.shape[dim] - width, stack.shape[dim], axis=dim)
        if swap and count == 2:
            first = lax.axis_index(axis) == 0
            incoming = lax.ppermute(jnp.where(first, tail, head), axis, [(0, 1), (1, 0)])
            nothing = jnp.zeros_like(incoming)
            from_left = jnp.where(first, nothing, incoming)
            from_right = jnp.where(first, incoming, nothing)
        else:
            from_left = lax.ppermute(tail, axis, [(i, i + 1) for i in range(count - 1)])
            from_right = lax.ppermute(head, axis, [(i + 1, i) for i in range(count - 1)])
        stack = jnp.concatenate([from_left, stack, from_right], axis=dim)
    return stack


def inside(shape, width):
    masks = []
    for axis, extent in zip(("gx", "gy", "gz"), shape):
        place = lax.axis_index(axis) * extent - width
        place = place + lax.broadcasted_iota(jnp.int32, (extent + 2 * width,), 0)
        masks.append((place >= 0) & (place < extent * lax.axis_size(axis)))
    return masks[0][:, None, None] & masks[1][None, :, None] & masks[2][None, None, :]


def crop(field, k):
    if k == 0:
        return field
    return field[k:-k, k:-k, k:-k]


def smooth_wide(start, source, diagonal, mask, steps):
    current = start
    for step in range(1, steps + 1):
        current = relax(current, crop(source, step), crop(diagonal, step))
        current = jnp.where(crop(mask, step), current, 0.0)
    return current


def coarser_level(source, damp):
    width = SWEEPS
    wide = exchange(jnp.stack([source, damp]), width, swap=True)
    wide_source = wide[0]
    wide_diag = 6.0 + wide[1]
    mask = inside(source.shape, width)
    start = jnp.where(mask, OMEGA * wide_source / wide_diag, 0.0)
    current = smooth_wide(start, wide_source, wide_diag, mask, SWEEPS - 1)
    return crop(current, 1), defect(current, source, 6.0 + damp)


def shards(right_side, initial_guess, damping, group_map, block_inverse):
    width = SWEEPS + 1
    wide = exchange(jnp.stack([initial_guess, right_side, damping]), width)
    wide_source = wide[1]
    wide_diag = 6.0 + wide[2]
    mask = inside(right_side.shape, width)
    current = smooth_wide(wide[0], wide_source, wide_diag, mask, SWEEPS)
    iterate = crop(current, 1)
    fine_defect = defect(current, right_side, 6.0 + damping)
    middle_damp = 4.0 * shrink(damping)
    middle_source = 4.0 * shrink(fine_defect)
    middle, middle_defect = coarser_level(middle_source, middle_damp)
    coarse_damp = 4.0 * shrink(middle_damp)
    coarse_source = 4.0 * shrink(middle_defect)
    coarse, coarse_defect = coarser_level(coarse_source, coarse_damp)
    cells = coarse_defect.size
    digits = DIGITS
    owner = group_map.reshape(cells, 1)
    letters = lax.broadcasted_iota(jnp.int32, (cells, digits), 1)
    high = (owner // digits == letters).astype(jnp.float32) * coarse_defect.reshape(cells, 1)
    low = (owner % digits == letters).astype(jnp.float32)
    partial_sums = lax.dot_general(
        high, low, (((0,), (0,)), ((), ())), precision=lax.Precision.HIGHEST
    ).reshape(NAGG)
    summed = lax.psum(partial_sums, "gz")
    summed = lax.psum(summed, "gx")
    splits = ((1, 4), (4, 4)) if lax.axis_size("gy") == 16 else ((1, lax.axis_size("gy")),)
    for stride, span in splits:
        groups = [
            [base + stride * k for k in range(span)]
            for base in range(lax.axis_size("gy"))
            if base % (stride * span) < stride
        ]
        summed = lax.psum(summed, "gy", axis_index_groups=groups)
    group_cells = (
        coarse_source.size * lax.axis_size("gx") * lax.axis_size("gy") * lax.axis_size("gz") // NAGG
    )
    aggregate_source = summed / math.sqrt(group_cells)
    solution = jnp.dot(block_inverse, aggregate_source, precision=lax.Precision.HIGHEST)
    return (iterate, middle, coarse, solution)


def solution(mesh):
    return jax.shard_map(
        shards,
        mesh=mesh,
        in_specs=(
            P("gx", "gy", "gz"),
            P("gx", "gy", "gz"),
            P("gx", "gy", "gz"),
            P("gx", "gy", "gz"),
            P("gy", None),
        ),
        out_specs=(P("gx", "gy", "gz"), P("gx", "gy", "gz"), P("gx", "gy", "gz"), P("gy")),
        check_vma=False,
    )
```

```python
import math

import jax
import jax.numpy as jnp
from jax import lax
from jax.sharding import PartitionSpec as P

SWEEPS = 4
NAGG = 1024
DIGITS = 32


OMEGA = 0.8


def with_halo(cells, sides, width):
    for axis, dim in sides:
        count = lax.axis_size(axis)
        ends = count - 1
        head = lax.slice_in_dim(cells, 0, width, axis=dim)
        tail = lax.slice_in_dim(cells, cells.shape[dim] - width, cells.shape[dim], axis=dim)
        cells = jnp.concatenate(
            [
                lax.ppermute(tail, axis, [(i, (i + 1) % count) for i in range(ends)]),
                cells,
                lax.ppermute(head, axis, [((i + 1) % count, i) for i in range(ends)]),
            ],
            axis=dim,
        )
    return cells


def neighbours(padded):
    total = padded[2:, 1:-1, 1:-1] + padded[:-2, 1:-1, 1:-1]
    total = total + padded[1:-1, 2:, 1:-1] + padded[1:-1, :-2, 1:-1]
    return total + padded[1:-1, 1:-1, 2:] + padded[1:-1, 1:-1, :-2]


def relax(padded, source, diagonal):
    centre = padded[1:-1, 1:-1, 1:-1]
    return centre + OMEGA * (source - (diagonal * centre - neighbours(padded))) / diagonal


def defect(padded, source, diagonal):
    centre = padded[1:-1, 1:-1, 1:-1]
    return source - (diagonal * centre - neighbours(padded))


def pair_matrix(rows, cols, along):
    row = lax.broadcasted_iota(jnp.int32, (rows, cols), 0)
    col = lax.broadcasted_iota(jnp.int32, (rows, cols), 1)
    if along == 0:
        return (col // 2 == row).astype(jnp.float32)
    return (row // 2 == col).astype(jnp.float32)


def shrink(field):
    extent_a, extent_b, extent_c = field.shape
    halves = field.reshape(extent_a // 2, 2, extent_b, extent_c)
    flat = (halves[:, 0] + halves[:, 1]).reshape(extent_a // 2 * extent_b, extent_c)
    rows = extent_a // 2 * extent_b
    flat = jnp.dot(pair_matrix(rows // 2, rows, 0), flat, precision=lax.Precision.HIGHEST)
    flat = jnp.dot(flat, pair_matrix(extent_c, extent_c // 2, 1), precision=lax.Precision.HIGHEST)
    return flat.reshape(extent_a // 2, extent_b // 2, extent_c // 2) * 0.125


def exchange(stack, width):
    for axis, dim in (("gx", 1), ("gz", 3), ("gy", 2)):
        count = lax.axis_size(axis)
        head = lax.slice_in_dim(stack, 0, width, axis=dim)
        tail = lax.slice_in_dim(stack, stack.shape[dim] - width, stack.shape[dim], axis=dim)
        stack = jnp.concatenate(
            [
                lax.ppermute(tail, axis, [(i, i + 1) for i in range(count - 1)]),
                stack,
                lax.ppermute(head, axis, [(i + 1, i) for i in range(count - 1)]),
            ],
            axis=dim,
        )
    return stack


def inside(shape, width):
    masks = []
    for axis, extent in zip(("gx", "gy", "gz"), shape):
        place = lax.axis_index(axis) * extent - width
        place = place + lax.broadcasted_iota(jnp.int32, (extent + 2 * width,), 0)
        masks.append((place >= 0) & (place < extent * lax.axis_size(axis)))
    return masks[0][:, None, None] & masks[1][None, :, None] & masks[2][None, None, :]


def crop(field, k):
    if k == 0:
        return field
    return field[k:-k, k:-k, k:-k]


def smooth_wide(start, source, diagonal, mask, steps):
    current = start
    for step in range(1, steps + 1):
        current = relax(current, crop(source, step), crop(diagonal, step))
        current = jnp.where(crop(mask, step), current, 0.0)
    return current


def coarser_level(source, damp):
    width = SWEEPS
    wide = exchange(jnp.stack([source, damp]), width)
    wide_source = wide[0]
    wide_diag = 6.0 + wide[1]
    mask = inside(source.shape, width)
    start = jnp.where(mask, OMEGA * wide_source / wide_diag, 0.0)
    current = smooth_wide(start, wide_source, wide_diag, mask, SWEEPS - 1)
    return crop(current, 1), defect(current, source, 6.0 + damp)


def shards(right_side, initial_guess, damping, group_map, block_inverse):
    width = SWEEPS + 1
    wide = exchange(jnp.stack([initial_guess, right_side, damping]), width)
    wide_source = wide[1]
    wide_diag = 6.0 + wide[2]
    mask = inside(right_side.shape, width)
    current = smooth_wide(wide[0], wide_source, wide_diag, mask, SWEEPS)
    iterate = crop(current, 1)
    fine_defect = defect(current, right_side, 6.0 + damping)
    middle_damp = 4.0 * shrink(damping)
    middle_source = 4.0 * shrink(fine_defect)
    middle, middle_defect = coarser_level(middle_source, middle_damp)
    coarse_damp = 4.0 * shrink(middle_damp)
    coarse_source = 4.0 * shrink(middle_defect)
    coarse, coarse_defect = coarser_level(coarse_source, coarse_damp)
    cells = coarse_defect.size
    digits = DIGITS
    owner = group_map.reshape(cells, 1)
    letters = lax.broadcasted_iota(jnp.int32, (cells, digits), 1)
    high = (owner // digits == letters).astype(jnp.float32) * coarse_defect.reshape(cells, 1)
    low = (owner % digits == letters).astype(jnp.float32)
    partial_sums = lax.dot_general(
        high, low, (((0,), (0,)), ((), ())), precision=lax.Precision.HIGHEST
    ).reshape(NAGG)
    summed = lax.psum(partial_sums, "gz")
    summed = lax.psum(summed, "gx")
    splits = ((1, 4), (4, 4)) if lax.axis_size("gy") == 16 else ((1, lax.axis_size("gy")),)
    for stride, span in splits:
        groups = [
            [base + stride * k for k in range(span)]
            for base in range(lax.axis_size("gy"))
            if base % (stride * span) < stride
        ]
        summed = lax.psum(summed, "gy", axis_index_groups=groups)
    group_cells = (
        coarse_source.size * lax.axis_size("gx") * lax.axis_size("gy") * lax.axis_size("gz") // NAGG
    )
    aggregate_source = summed / math.sqrt(group_cells)
    solution = jnp.dot(block_inverse, aggregate_source, precision=lax.Precision.HIGHEST)
    return (iterate, middle, coarse, solution)


def solution(mesh):
    return jax.shard_map(
        shards,
        mesh=mesh,
        in_specs=(
            P("gx", "gy", "gz"),
            P("gx", "gy", "gz"),
            P("gx", "gy", "gz"),
            P("gx", "gy", "gz"),
            P("gy", None),
        ),
        out_specs=(P("gx", "gy", "gz"), P("gx", "gy", "gz"), P("gx", "gy", "gz"), P("gy")),
        check_vma=False,
    )
```

```python
import math

import jax
import jax.numpy as jnp
from jax import lax
from jax.sharding import PartitionSpec as P

SWEEPS = 4
NAGG = 1024
DIGITS = 32


OMEGA = 0.8


def with_halo(cells, sides, width):
    for axis, dim in sides:
        count = lax.axis_size(axis)
        ends = count - 1
        head = lax.slice_in_dim(cells, 0, width, axis=dim)
        tail = lax.slice_in_dim(cells, cells.shape[dim] - width, cells.shape[dim], axis=dim)
        cells = jnp.concatenate(
            [
                lax.ppermute(tail, axis, [(i, (i + 1) % count) for i in range(ends)]),
                cells,
                lax.ppermute(head, axis, [((i + 1) % count, i) for i in range(ends)]),
            ],
            axis=dim,
        )
    return cells


def neighbours(padded):
    total = padded[2:, 1:-1, 1:-1] + padded[:-2, 1:-1, 1:-1]
    total = total + padded[1:-1, 2:, 1:-1] + padded[1:-1, :-2, 1:-1]
    return total + padded[1:-1, 1:-1, 2:] + padded[1:-1, 1:-1, :-2]


def relax(padded, source, diagonal):
    centre = padded[1:-1, 1:-1, 1:-1]
    return centre + OMEGA * (source - (diagonal * centre - neighbours(padded))) / diagonal


def defect(padded, source, diagonal):
    centre = padded[1:-1, 1:-1, 1:-1]
    return source - (diagonal * centre - neighbours(padded))


def pair_matrix(rows, cols, along):
    row = lax.broadcasted_iota(jnp.int32, (rows, cols), 0)
    col = lax.broadcasted_iota(jnp.int32, (rows, cols), 1)
    if along == 0:
        return (col // 2 == row).astype(jnp.float32)
    return (row // 2 == col).astype(jnp.float32)


def shrink(field):
    extent_a, extent_b, extent_c = field.shape
    halves = field.reshape(extent_a // 2, 2, extent_b, extent_c)
    flat = (halves[:, 0] + halves[:, 1]).reshape(extent_a // 2 * extent_b, extent_c)
    rows = extent_a // 2 * extent_b
    flat = jnp.dot(pair_matrix(rows // 2, rows, 0), flat, precision=lax.Precision.HIGHEST)
    flat = jnp.dot(flat, pair_matrix(extent_c, extent_c // 2, 1), precision=lax.Precision.HIGHEST)
    return flat.reshape(extent_a // 2, extent_b // 2, extent_c // 2) * 0.125


def shipped(full, thin, axis, pairs):
    fields, width = full.shape[0], full.shape[1]
    rest = full.shape[2:]
    packed = jnp.concatenate(
        [full.reshape((fields * width,) + rest), thin.reshape((-1,) + rest)], axis=0
    )
    packed = lax.ppermute(packed, axis, pairs)
    return packed[: fields * width].reshape(full.shape), packed[fields * width :].reshape(thin.shape)


def exchange(stack, width, narrow=0):
    for axis, dim in (("gx", 1), ("gy", 2), ("gz", 3)):
        count = lax.axis_size(axis)
        forward = [(i, i + 1) for i in range(count - 1)]
        backward = [(i + 1, i) for i in range(count - 1)]
        if narrow and dim == 1:
            keep = stack.shape[0] - narrow
            full, thin = stack[:keep], stack[keep:]
            edge = ((0, 0), (1, 0), (0, 0), (0, 0))
            left_full, left_thin = shipped(full[:, -width:], thin[:, 1 - width :], axis, forward)
            right_full, right_thin = shipped(full[:, :width], thin[:, : width - 1], axis, backward)
            from_left = jnp.concatenate([left_full, jnp.pad(left_thin, edge)], axis=0)
            from_right = jnp.concatenate([right_full, jnp.pad(right_thin, edge[:1] + ((0, 1),) + edge[2:])], axis=0)
        else:
            head = lax.slice_in_dim(stack, 0, width, axis=dim)
            tail = lax.slice_in_dim(stack, stack.shape[dim] - width, stack.shape[dim], axis=dim)
            from_left = lax.ppermute(tail, axis, forward)
            from_right = lax.ppermute(head, axis, backward)
        stack = jnp.concatenate([from_left, stack, from_right], axis=dim)
    return stack


def inside(shape, width):
    masks = []
    for axis, extent in zip(("gx", "gy", "gz"), shape):
        place = lax.axis_index(axis) * extent - width
        place = place + lax.broadcasted_iota(jnp.int32, (extent + 2 * width,), 0)
        masks.append((place >= 0) & (place < extent * lax.axis_size(axis)))
    return masks[0][:, None, None] & masks[1][None, :, None] & masks[2][None, None, :]


def crop(field, k):
    if k == 0:
        return field
    return field[k:-k, k:-k, k:-k]


def smooth_wide(start, source, diagonal, mask, steps):
    current = start
    for step in range(1, steps + 1):
        current = relax(current, crop(source, step), crop(diagonal, step))
        current = jnp.where(crop(mask, step), current, 0.0)
    return current


def coarser_level(source, damp):
    width = SWEEPS
    wide = exchange(jnp.stack([source, damp]), width)
    wide_source = wide[0]
    wide_diag = 6.0 + wide[1]
    mask = inside(source.shape, width)
    start = jnp.where(mask, OMEGA * wide_source / wide_diag, 0.0)
    current = smooth_wide(start, wide_source, wide_diag, mask, SWEEPS - 1)
    return crop(current, 1), defect(current, source, 6.0 + damp)


def shards(right_side, initial_guess, damping, group_map, block_inverse):
    width = SWEEPS + 1
    wide = exchange(jnp.stack([initial_guess, right_side, damping]), width, narrow=2)
    wide_source = wide[1]
    wide_diag = 6.0 + wide[2]
    mask = inside(right_side.shape, width)
    current = smooth_wide(wide[0], wide_source, wide_diag, mask, SWEEPS)
    iterate = crop(current, 1)
    fine_defect = defect(current, right_side, 6.0 + damping)
    middle_damp = 4.0 * shrink(damping)
    middle_source = 4.0 * shrink(fine_defect)
    middle, middle_defect = coarser_level(middle_source, middle_damp)
    coarse_damp = 4.0 * shrink(middle_damp)
    coarse_source = 4.0 * shrink(middle_defect)
    coarse, coarse_defect = coarser_level(coarse_source, coarse_damp)
    cells = coarse_defect.size
    digits = DIGITS
    owner = group_map.reshape(cells, 1)
    letters = lax.broadcasted_iota(jnp.int32, (cells, digits), 1)
    high = (owner // digits == letters).astype(jnp.float32) * coarse_defect.reshape(cells, 1)
    low = (owner % digits == letters).astype(jnp.float32)
    partial_sums = lax.dot_general(
        high, low, (((0,), (0,)), ((), ())), precision=lax.Precision.HIGHEST
    ).reshape(NAGG)
    summed = lax.psum(partial_sums, "gz")
    summed = lax.psum(summed, "gx")
    splits = ((1, 4), (4, 4)) if lax.axis_size("gy") == 16 else ((1, lax.axis_size("gy")),)
    for stride, span in splits:
        groups = [
            [base + stride * k for k in range(span)]
            for base in range(lax.axis_size("gy"))
            if base % (stride * span) < stride
        ]
        summed = lax.psum(summed, "gy", axis_index_groups=groups)
    group_cells = (
        coarse_source.size * lax.axis_size("gx") * lax.axis_size("gy") * lax.axis_size("gz") // NAGG
    )
    aggregate_source = summed / math.sqrt(group_cells)
    solution = jnp.dot(block_inverse, aggregate_source, precision=lax.Precision.HIGHEST)
    return (iterate, middle, coarse, solution)


def solution(mesh):
    return jax.shard_map(
        shards,
        mesh=mesh,
        in_specs=(
            P("gx", "gy", "gz"),
            P("gx", "gy", "gz"),
            P("gx", "gy", "gz"),
            P("gx", "gy", "gz"),
            P("gy", None),
        ),
        out_specs=(P("gx", "gy", "gz"), P("gx", "gy", "gz"), P("gx", "gy", "gz"), P("gy")),
        check_vma=False,
    )
```

```python
import math

import jax
import jax.numpy as jnp
from jax import lax
from jax.sharding import PartitionSpec as P

SWEEPS = 4
NAGG = 1024
DIGITS = 32


OMEGA = 0.8


def with_halo(cells, sides, width):
    for axis, dim in sides:
        count = lax.axis_size(axis)
        ends = count - 1
        head = lax.slice_in_dim(cells, 0, width, axis=dim)
        tail = lax.slice_in_dim(cells, cells.shape[dim] - width, cells.shape[dim], axis=dim)
        cells = jnp.concatenate(
            [
                lax.ppermute(tail, axis, [(i, (i + 1) % count) for i in range(ends)]),
                cells,
                lax.ppermute(head, axis, [((i + 1) % count, i) for i in range(ends)]),
            ],
            axis=dim,
        )
    return cells


def neighbours(padded):
    total = padded[2:, 1:-1, 1:-1] + padded[:-2, 1:-1, 1:-1]
    total = total + padded[1:-1, 2:, 1:-1] + padded[1:-1, :-2, 1:-1]
    return total + padded[1:-1, 1:-1, 2:] + padded[1:-1, 1:-1, :-2]


def relax(padded, source, diagonal):
    centre = padded[1:-1, 1:-1, 1:-1]
    return centre + OMEGA * (source - (diagonal * centre - neighbours(padded))) / diagonal


def defect(padded, source, diagonal):
    centre = padded[1:-1, 1:-1, 1:-1]
    return source - (diagonal * centre - neighbours(padded))


def pair_matrix(rows, cols, along):
    row = lax.broadcasted_iota(jnp.int32, (rows, cols), 0)
    col = lax.broadcasted_iota(jnp.int32, (rows, cols), 1)
    if along == 0:
        return (col // 2 == row).astype(jnp.float32)
    return (row // 2 == col).astype(jnp.float32)


def shrink(field):
    extent_a, extent_b, extent_c = field.shape
    halves = field.reshape(extent_a // 2, 2, extent_b, extent_c)
    flat = (halves[:, 0] + halves[:, 1]).reshape(extent_a // 2 * extent_b, extent_c)
    rows = extent_a // 2 * extent_b
    flat = jnp.dot(pair_matrix(rows // 2, rows, 0), flat, precision=lax.Precision.HIGHEST)
    flat = jnp.dot(flat, pair_matrix(extent_c, extent_c // 2, 1), precision=lax.Precision.HIGHEST)
    return flat.reshape(extent_a // 2, extent_b // 2, extent_c // 2) * 0.125


def exchange(stack, width):
    for axis, dim in (("gx", 1), ("gy", 2), ("gz", 3)):
        count = lax.axis_size(axis)
        head = lax.slice_in_dim(stack, 0, width, axis=dim)
        tail = lax.slice_in_dim(stack, stack.shape[dim] - width, stack.shape[dim], axis=dim)
        stack = jnp.concatenate(
            [
                lax.ppermute(tail, axis, [(i, i + 1) for i in range(count - 1)]),
                stack,
                lax.ppermute(head, axis, [(i + 1, i) for i in range(count - 1)]),
            ],
            axis=dim,
        )
    return stack


def inside(shape, width):
    masks = []
    for axis, extent in zip(("gx", "gy", "gz"), shape):
        place = lax.axis_index(axis) * extent - width
        place = place + lax.broadcasted_iota(jnp.int32, (extent + 2 * width,), 0)
        masks.append((place >= 0) & (place < extent * lax.axis_size(axis)))
    return masks[0][:, None, None] & masks[1][None, :, None] & masks[2][None, None, :]


def crop(field, k):
    if k == 0:
        return field
    return field[k:-k, k:-k, k:-k]


def smooth_wide(start, source, diagonal, mask, steps):
    current = start
    for step in range(1, steps + 1):
        current = relax(current, crop(source, step), crop(diagonal, step))
        current = jnp.where(crop(mask, step), current, 0.0)
    return current


def coarser_level(source, damp):
    width = SWEEPS
    wide = exchange(jnp.stack([source, damp]), width)
    wide_source = wide[0]
    wide_diag = 6.0 + wide[1]
    mask = inside(source.shape, width)
    start = jnp.where(mask, OMEGA * wide_source / wide_diag, 0.0)
    current = smooth_wide(start, wide_source, wide_diag, mask, SWEEPS - 1)
    return crop(current, 1), defect(current, source, 6.0 + damp)


def shards(right_side, initial_guess, damping, group_map, block_inverse):
    width = SWEEPS + 1
    wide = exchange(jnp.stack([initial_guess, right_side, damping]), width)
    wide_source = wide[1]
    wide_diag = 6.0 + wide[2]
    mask = inside(right_side.shape, width)
    current = smooth_wide(wide[0], wide_source, wide_diag, mask, SWEEPS)
    iterate = crop(current, 1)
    fine_defect = defect(current, right_side, 6.0 + damping)
    middle_damp = 4.0 * shrink(damping)
    middle_source = 4.0 * shrink(fine_defect)
    middle, middle_defect = coarser_level(middle_source, middle_damp)
    coarse_damp = 4.0 * shrink(middle_damp)
    coarse_source = 4.0 * shrink(middle_defect)
    coarse, coarse_defect = coarser_level(coarse_source, coarse_damp)
    cells = coarse_defect.size
    digits = DIGITS
    owner = group_map.reshape(cells, 1)
    letters = lax.broadcasted_iota(jnp.int32, (cells, digits), 1)
    high = (owner // digits == letters).astype(jnp.float32) * coarse_defect.reshape(cells, 1)
    low = (owner % digits == letters).astype(jnp.float32)
    partial_sums = lax.dot_general(
        high, low, (((0,), (0,)), ((), ())), precision=lax.Precision.HIGHEST
    ).reshape(NAGG)
    summed = lax.psum(partial_sums, "gx")
    if lax.axis_size("gy") == 16:
        depth = lax.axis_size("gz")
        column = [[(base + j) * depth + z for j in range(4) for z in range(depth)] for base in range(0, 16, 4)]
        summed = lax.psum(summed, ("gy", "gz"), axis_index_groups=column)
        rows = [[base + 4 * k for k in range(4)] for base in range(4)]
        summed = lax.psum(summed, "gy", axis_index_groups=rows)
    else:
        summed = lax.psum(summed, ("gy", "gz"))
    group_cells = (
        coarse_source.size * lax.axis_size("gx") * lax.axis_size("gy") * lax.axis_size("gz") // NAGG
    )
    aggregate_source = summed / math.sqrt(group_cells)
    solution = jnp.dot(block_inverse, aggregate_source, precision=lax.Precision.HIGHEST)
    return (iterate, middle, coarse, solution)


def solution(mesh):
    return jax.shard_map(
        shards,
        mesh=mesh,
        in_specs=(
            P("gx", "gy", "gz"),
            P("gx", "gy", "gz"),
            P("gx", "gy", "gz"),
            P("gx", "gy", "gz"),
            P("gy", None),
        ),
        out_specs=(P("gx", "gy", "gz"), P("gx", "gy", "gz"), P("gx", "gy", "gz"), P("gy")),
        check_vma=False,
    )
```

```python
import math

import jax
import jax.numpy as jnp
from jax import lax
from jax.sharding import PartitionSpec as P

SWEEPS = 4
NAGG = 1024
DIGITS = 32


OMEGA = 0.8


def with_halo(cells, sides, width):
    for axis, dim in sides:
        count = lax.axis_size(axis)
        ends = count - 1
        head = lax.slice_in_dim(cells, 0, width, axis=dim)
        tail = lax.slice_in_dim(cells, cells.shape[dim] - width, cells.shape[dim], axis=dim)
        cells = jnp.concatenate(
            [
                lax.ppermute(tail, axis, [(i, (i + 1) % count) for i in range(ends)]),
                cells,
                lax.ppermute(head, axis, [((i + 1) % count, i) for i in range(ends)]),
            ],
            axis=dim,
        )
    return cells


def neighbours(padded):
    total = padded[2:, 1:-1, 1:-1] + padded[:-2, 1:-1, 1:-1]
    total = total + padded[1:-1, 2:, 1:-1] + padded[1:-1, :-2, 1:-1]
    return total + padded[1:-1, 1:-1, 2:] + padded[1:-1, 1:-1, :-2]


def relax(padded, source, diagonal):
    centre = padded[1:-1, 1:-1, 1:-1]
    return centre + OMEGA * (source - (diagonal * centre - neighbours(padded))) / diagonal


def defect(padded, source, diagonal):
    centre = padded[1:-1, 1:-1, 1:-1]
    return source - (diagonal * centre - neighbours(padded))


def pair_matrix(rows, cols, along):
    row = lax.broadcasted_iota(jnp.int32, (rows, cols), 0)
    col = lax.broadcasted_iota(jnp.int32, (rows, cols), 1)
    if along == 0:
        return (col // 2 == row).astype(jnp.float32)
    return (row // 2 == col).astype(jnp.float32)


def shrink(field):
    extent_a, extent_b, extent_c = field.shape
    halves = field.reshape(extent_a // 2, 2, extent_b, extent_c)
    flat = (halves[:, 0] + halves[:, 1]).reshape(extent_a // 2 * extent_b, extent_c)
    rows = extent_a // 2 * extent_b
    flat = jnp.dot(pair_matrix(rows // 2, rows, 0), flat, precision=lax.Precision.HIGHEST)
    flat = jnp.dot(flat, pair_matrix(extent_c, extent_c // 2, 1), precision=lax.Precision.HIGHEST)
    return flat.reshape(extent_a // 2, extent_b // 2, extent_c // 2) * 0.125


def exchange(stack, width, order=(("gx", 1), ("gy", 2), ("gz", 3))):
    for axis, dim in order:
        count = lax.axis_size(axis)
        head = lax.slice_in_dim(stack, 0, width, axis=dim)
        tail = lax.slice_in_dim(stack, stack.shape[dim] - width, stack.shape[dim], axis=dim)
        stack = jnp.concatenate(
            [
                lax.ppermute(tail, axis, [(i, i + 1) for i in range(count - 1)]),
                stack,
                lax.ppermute(head, axis, [(i + 1, i) for i in range(count - 1)]),
            ],
            axis=dim,
        )
    return stack


def inside(shape, width):
    masks = []
    for axis, extent in zip(("gx", "gy", "gz"), shape):
        place = lax.axis_index(axis) * extent - width
        place = place + lax.broadcasted_iota(jnp.int32, (extent + 2 * width,), 0)
        masks.append((place >= 0) & (place < extent * lax.axis_size(axis)))
    return masks[0][:, None, None] & masks[1][None, :, None] & masks[2][None, None, :]


def crop(field, k):
    if k == 0:
        return field
    return field[k:-k, k:-k, k:-k]


def smooth_wide(start, source, diagonal, mask, steps):
    current = start
    for step in range(1, steps + 1):
        current = relax(current, crop(source, step), crop(diagonal, step))
        current = jnp.where(crop(mask, step), current, 0.0)
    return current


def coarser_level(source, damp, order):
    width = SWEEPS
    wide = exchange(jnp.stack([source, damp]), width, order)
    wide_source = wide[0]
    wide_diag = 6.0 + wide[1]
    mask = inside(source.shape, width)
    start = jnp.where(mask, OMEGA * wide_source / wide_diag, 0.0)
    current = smooth_wide(start, wide_source, wide_diag, mask, SWEEPS - 1)
    return crop(current, 1), defect(current, source, 6.0 + damp)


def shards(right_side, initial_guess, damping, group_map, block_inverse):
    width = SWEEPS + 1
    wide = exchange(jnp.stack([initial_guess, right_side, damping]), width)
    wide_source = wide[1]
    wide_diag = 6.0 + wide[2]
    mask = inside(right_side.shape, width)
    current = smooth_wide(wide[0], wide_source, wide_diag, mask, SWEEPS)
    iterate = crop(current, 1)
    fine_defect = defect(current, right_side, 6.0 + damping)
    middle_damp = 4.0 * shrink(damping)
    middle_source = 4.0 * shrink(fine_defect)
    middle, middle_defect = coarser_level(middle_source, middle_damp, (("gx", 1), ("gy", 2), ("gz", 3)))
    coarse_damp = 4.0 * shrink(middle_damp)
    coarse_source = 4.0 * shrink(middle_defect)
    coarse, coarse_defect = coarser_level(coarse_source, coarse_damp, (("gz", 3), ("gy", 2), ("gx", 1)))
    cells = coarse_defect.size
    digits = DIGITS
    owner = group_map.reshape(cells, 1)
    letters = lax.broadcasted_iota(jnp.int32, (cells, digits), 1)
    high = (owner // digits == letters).astype(jnp.float32) * coarse_defect.reshape(cells, 1)
    low = (owner % digits == letters).astype(jnp.float32)
    partial_sums = lax.dot_general(
        high, low, (((0,), (0,)), ((), ())), precision=lax.Precision.HIGHEST
    ).reshape(NAGG)
    summed = lax.psum(partial_sums, "gz")
    summed = lax.psum(summed, "gx")
    splits = ((1, 4), (4, 4)) if lax.axis_size("gy") == 16 else ((1, lax.axis_size("gy")),)
    for stride, span in splits:
        groups = [
            [base + stride * k for k in range(span)]
            for base in range(lax.axis_size("gy"))
            if base % (stride * span) < stride
        ]
        summed = lax.psum(summed, "gy", axis_index_groups=groups)
    group_cells = (
        coarse_source.size * lax.axis_size("gx") * lax.axis_size("gy") * lax.axis_size("gz") // NAGG
    )
    aggregate_source = summed / math.sqrt(group_cells)
    solution = jnp.dot(block_inverse, aggregate_source, precision=lax.Precision.HIGHEST)
    return (iterate, middle, coarse, solution)


def solution(mesh):
    return jax.shard_map(
        shards,
        mesh=mesh,
        in_specs=(
            P("gx", "gy", "gz"),
            P("gx", "gy", "gz"),
            P("gx", "gy", "gz"),
            P("gx", "gy", "gz"),
            P("gy", None),
        ),
        out_specs=(P("gx", "gy", "gz"), P("gx", "gy", "gz"), P("gx", "gy", "gz"), P("gy")),
        check_vma=False,
    )
```

```python
import math

import jax
import jax.numpy as jnp
from jax import lax
from jax.sharding import PartitionSpec as P

SWEEPS = 4
NAGG = 1024
DIGITS = 32


OMEGA = 0.8


def with_halo(cells, sides, width):
    for axis, dim in sides:
        count = lax.axis_size(axis)
        ends = count - 1
        head = lax.slice_in_dim(cells, 0, width, axis=dim)
        tail = lax.slice_in_dim(cells, cells.shape[dim] - width, cells.shape[dim], axis=dim)
        cells = jnp.concatenate(
            [
                lax.ppermute(tail, axis, [(i, (i + 1) % count) for i in range(ends)]),
                cells,
                lax.ppermute(head, axis, [((i + 1) % count, i) for i in range(ends)]),
            ],
            axis=dim,
        )
    return cells


def neighbours(padded):
    total = padded[2:, 1:-1, 1:-1] + padded[:-2, 1:-1, 1:-1]
    total = total + padded[1:-1, 2:, 1:-1] + padded[1:-1, :-2, 1:-1]
    return total + padded[1:-1, 1:-1, 2:] + padded[1:-1, 1:-1, :-2]


def relax(padded, source, diagonal):
    centre = padded[1:-1, 1:-1, 1:-1]
    return centre + OMEGA * (source - (diagonal * centre - neighbours(padded))) / diagonal


def defect(padded, source, diagonal):
    centre = padded[1:-1, 1:-1, 1:-1]
    return source - (diagonal * centre - neighbours(padded))


def pair_matrix(rows, cols, along):
    row = lax.broadcasted_iota(jnp.int32, (rows, cols), 0)
    col = lax.broadcasted_iota(jnp.int32, (rows, cols), 1)
    if along == 0:
        return (col // 2 == row).astype(jnp.float32)
    return (row // 2 == col).astype(jnp.float32)


def shrink(field):
    extent_a, extent_b, extent_c = field.shape
    halves = field.reshape(extent_a // 2, 2, extent_b, extent_c)
    flat = (halves[:, 0] + halves[:, 1]).reshape(extent_a // 2 * extent_b, extent_c)
    rows = extent_a // 2 * extent_b
    flat = jnp.dot(pair_matrix(rows // 2, rows, 0), flat, precision=lax.Precision.HIGHEST)
    flat = jnp.dot(flat, pair_matrix(extent_c, extent_c // 2, 1), precision=lax.Precision.HIGHEST)
    return flat.reshape(extent_a // 2, extent_b // 2, extent_c // 2) * 0.125


def exchange(stack, width, order=(("gx", 1), ("gy", 2), ("gz", 3))):
    for axis, dim in order:
        count = lax.axis_size(axis)
        head = lax.slice_in_dim(stack, 0, width, axis=dim)
        tail = lax.slice_in_dim(stack, stack.shape[dim] - width, stack.shape[dim], axis=dim)
        stack = jnp.concatenate(
            [
                lax.ppermute(tail, axis, [(i, i + 1) for i in range(count - 1)]),
                stack,
                lax.ppermute(head, axis, [(i + 1, i) for i in range(count - 1)]),
            ],
            axis=dim,
        )
    return stack


def inside(shape, width):
    masks = []
    for axis, extent in zip(("gx", "gy", "gz"), shape):
        place = lax.axis_index(axis) * extent - width
        place = place + lax.broadcasted_iota(jnp.int32, (extent + 2 * width,), 0)
        masks.append((place >= 0) & (place < extent * lax.axis_size(axis)))
    return masks[0][:, None, None] & masks[1][None, :, None] & masks[2][None, None, :]


def crop(field, k):
    if k == 0:
        return field
    return field[k:-k, k:-k, k:-k]


def smooth_wide(start, source, diagonal, mask, steps):
    current = start
    for step in range(1, steps + 1):
        current = relax(current, crop(source, step), crop(diagonal, step))
        current = jnp.where(crop(mask, step), current, 0.0)
    return current


def coarser_level(source, damp, order):
    width = SWEEPS
    wide = exchange(jnp.stack([source, damp]), width, order)
    wide_source = wide[0]
    wide_diag = 6.0 + wide[1]
    mask = inside(source.shape, width)
    start = jnp.where(mask, OMEGA * wide_source / wide_diag, 0.0)
    current = smooth_wide(start, wide_source, wide_diag, mask, SWEEPS - 1)
    return crop(current, 1), defect(current, source, 6.0 + damp)


def shards(right_side, initial_guess, damping, group_map, block_inverse):
    width = SWEEPS + 1
    wide = exchange(jnp.stack([initial_guess, right_side, damping]), width)
    wide_source = wide[1]
    wide_diag = 6.0 + wide[2]
    mask = inside(right_side.shape, width)
    current = smooth_wide(wide[0], wide_source, wide_diag, mask, SWEEPS)
    iterate = crop(current, 1)
    fine_defect = defect(current, right_side, 6.0 + damping)
    middle_damp = 4.0 * shrink(damping)
    middle_source = 4.0 * shrink(fine_defect)
    middle, middle_defect = coarser_level(middle_source, middle_damp, (("gx", 1), ("gy", 2), ("gz", 3)))
    coarse_damp = 4.0 * shrink(middle_damp)
    coarse_source = 4.0 * shrink(middle_defect)
    coarse, coarse_defect = coarser_level(coarse_source, coarse_damp, (("gz", 3), ("gx", 1), ("gy", 2)))
    cells = coarse_defect.size
    digits = DIGITS
    owner = group_map.reshape(cells, 1)
    letters = lax.broadcasted_iota(jnp.int32, (cells, digits), 1)
    high = (owner // digits == letters).astype(jnp.float32) * coarse_defect.reshape(cells, 1)
    low = (owner % digits == letters).astype(jnp.float32)
    partial_sums = lax.dot_general(
        high, low, (((0,), (0,)), ((), ())), precision=lax.Precision.HIGHEST
    ).reshape(NAGG)
    summed = lax.psum(partial_sums, "gz")
    summed = lax.psum(summed, "gx")
    splits = ((1, 4), (4, 4)) if lax.axis_size("gy") == 16 else ((1, lax.axis_size("gy")),)
    for stride, span in splits:
        groups = [
            [base + stride * k for k in range(span)]
            for base in range(lax.axis_size("gy"))
            if base % (stride * span) < stride
        ]
        summed = lax.psum(summed, "gy", axis_index_groups=groups)
    group_cells = (
        coarse_source.size * lax.axis_size("gx") * lax.axis_size("gy") * lax.axis_size("gz") // NAGG
    )
    aggregate_source = summed / math.sqrt(group_cells)
    solution = jnp.dot(block_inverse, aggregate_source, precision=lax.Precision.HIGHEST)
    return (iterate, middle, coarse, solution)


def solution(mesh):
    return jax.shard_map(
        shards,
        mesh=mesh,
        in_specs=(
            P("gx", "gy", "gz"),
            P("gx", "gy", "gz"),
            P("gx", "gy", "gz"),
            P("gx", "gy", "gz"),
            P("gy", None),
        ),
        out_specs=(P("gx", "gy", "gz"), P("gx", "gy", "gz"), P("gx", "gy", "gz"), P("gy")),
        check_vma=False,
    )
```
